32 devices in a mesh: seq: 8 (over z, x), ch: 4 (over y, core).
Axes of the slice: x: 2, y: 2, z: 4, core: 2. Of those that a mesh axis runs over, the one named last changes fastest.
Arguments:
- tokens: int32 [2, 4096], P(None, 'seq'), may hold values from 0 to 3
- masked: int32 [2, 4096], P(None, 'seq'), may hold values 0 or 1
- hidden_forward: bfloat16 [2, 4096, 1024], P(None, 'seq', 'ch'), may hold values from -16 to 16
- hidden_reverse: bfloat16 [2, 4096, 1024], P(None, 'seq', 'ch'), may hold values from -16 to 16
- embed_table: bfloat16 [5, 1024], P(None, 'ch'), may hold values from -3 to 3
- conv_kernel: float32 [7, 1024], P(None, 'ch'), may hold values from -2.4 to 2.4
- conv_bias: float32 [1024], P('ch'), may hold values from -3 to 3
- norm_gain: float32 [1024], P('ch'), may hold values from 0.25 to 1.75
- w_gate: bfloat16 [1024, 4096], P(None, 'ch'), may hold values from -0.1875 to 0.1875
- w_value: bfloat16 [1024, 4096], P(None, 'ch'), may hold values from -0.1875 to 0.1875
- w_out: bfloat16 [4096, 1024], P('ch'), may hold values from -0.09375 to 0.09375
Outputs:
- out_forward: bfloat16 [2, 4096, 1024], P(None, 'seq', 'ch')
- out_reverse: bfloat16 [2, 4096, 1024], P(None, 'seq', 'ch')
The draws below stay inside these ranges and needn't reach their ends.
Inputs may be any that keep to these rules, and one draw needn't show every extreme that they name: `tokens`: base ids A, C, G, T are 0, 1, 2, 3 and the complement of b is 3 - b.
All inputs are finite; a program needn't handle non-finite values. No bound on the sum of `masked` on one device may be relied on, other than what follows from the above.
Results may differ from the reference program's by a relative error of at most 0.0067.
Values may be sent and summed in bfloat16 or wider, within the bound.
No kernel may reach another device: no remote copies, remote signals or barrier semaphores. Data moves between devices by JAX's collectives and lax.ppermute only.
A program may use at most 128 MiB of HBM per device.

```python
import jax
import jax.numpy as jnp
from jax import lax

D = 1024
FF = 4096
KSIZE = 7
VOCAB = 5
SEQS = 2
BASES_DEV = 512
SEQLEN = 4096


def draw_stream(key, marker):
    key_base = jax.random.fold_in(key, marker)
    key_values = jax.random.fold_in(key_base, 1)
    key_factor = jax.random.fold_in(key_base, 2)
    column = jnp.arange(D, dtype=jnp.float32) / (D - 1)
    factor = jax.random.uniform(key_factor, (D,), jnp.float32, 0.7, 1.3)
    channel_scale = 0.3 * jnp.power(10.0, column) * factor
    values = jnp.clip(jax.random.normal(key_values, (SEQS, SEQLEN, D), jnp.float32), -4.0, 4.0)
    return (values * channel_scale).astype(jnp.bfloat16)


def draw_hidden_forward(key, part):
    return draw_stream(key, 11)


def draw_hidden_reverse(key, part):
    return draw_stream(key, 23)


def place_ends(drawn, own_key, low, high):
    extent = drawn.shape
    spot = [jax.random.randint(jax.random.fold_in(own_key, axis), (), 0, extent[axis]) for axis in range(len(extent))]
    drawn = drawn.at[tuple(spot)].set(low)
    longest = extent.index(max(extent))
    spot[longest] = (spot[longest] + 1) % extent[longest]
    return drawn.at[tuple(spot)].set(high)


def shard_levels(key, extent, cuts, low, largest):
    gain, own = 1.0, jax.random.fold_in(key, 6)
    for axis_at, parts in cuts:
        steps = jnp.exp(jax.random.uniform(jax.random.fold_in(own, axis_at), (parts,), jnp.float32, low / len(cuts), largest / len(cuts)))
        gain = gain * jnp.repeat(steps, extent[axis_at] // parts).reshape([-1 if axis == axis_at else 1 for axis in range(len(extent))])
    return gain


def gaussian(stream_key, extent, scale, bound, cuts=(), kind=jnp.bfloat16):
    entries = jax.random.normal(stream_key, extent, jnp.float32) * scale
    if len(cuts) > 0:
        entries = shard_levels(stream_key, extent, cuts, -0.22, 0.18) * entries
    return jnp.clip(entries, min=-bound, max=bound).astype(kind)


def setup_inputs(seed: int = 0) -> dict:
    key_list = jax.random.split(jax.random.key(seed), 12)
    tokens = place_ends(jax.random.randint(key_list[0], (SEQS, SEQLEN), 0, 4), jax.random.fold_in(key_list[0], 1), 0, 3).astype(jnp.int32)
    masked = place_ends((jax.random.randint(key_list[1], (SEQS, SEQLEN), 0, 4) < 1).astype(jnp.int32), jax.random.fold_in(key_list[1], 1), 0, 1)
    hidden_forward = draw_hidden_forward(jax.random.fold_in(key_list[11], 71), 0)
    hidden_reverse = draw_hidden_reverse(jax.random.fold_in(key_list[11], 71), 0)
    embed_table = gaussian(key_list[4], (VOCAB, D), 0.5, 3.0, ((1, 4),))
    conv_kernel = gaussian(key_list[5], (KSIZE, D), 0.4, 2.4, ((1, 4),), jnp.float32)
    conv_bias = gaussian(key_list[6], (D,), 0.5, 3.0, ((0, 4),), jnp.float32)
    norm_gain = jnp.clip(1.0 + 0.15 * jax.random.normal(key_list[7], (D,), jnp.float32), 0.25, 1.75)
    w_gate = gaussian(key_list[8], (D, FF), D ** -0.5, 0.1875, ((1, 4),))
    w_value = gaussian(key_list[9], (D, FF), D ** -0.5, 0.1875, ((1, 4),))
    w_out = gaussian(key_list[10], (FF, D), FF ** -0.5, 0.09375, ((0, 4),))
    return dict(tokens=tokens, masked=masked, hidden_forward=hidden_forward, hidden_reverse=hidden_reverse, embed_table=embed_table, conv_kernel=conv_kernel, conv_bias=conv_bias, norm_gain=norm_gain, w_gate=w_gate, w_value=w_value, w_out=w_out)


def rms_normed(values, norm_gain):
    mean_square = lax.optimization_barrier(jnp.mean(values * values, axis=-1, keepdims=True))
    return (values * lax.rsqrt(mean_square + 1e-05) * norm_gain).astype(jnp.bfloat16)

def depthwise(normed, conv_kernel, conv_bias):
    half_width = KSIZE // 2
    length = normed.shape[1]
    padded = jnp.pad(normed.astype(jnp.float32), ((0, 0), (half_width, half_width), (0, 0)))
    result = jnp.zeros(normed.shape, jnp.float32) + conv_bias
    for offset in range(KSIZE):
        result = result + conv_kernel[offset] * padded[:, offset:offset + length]
    return result.astype(jnp.bfloat16)

def pointwise(conv_out, w_gate, w_value, w_out):
    blocks = conv_out.reshape(-1, BASES_DEV, D)

    def one_block(block):
        gate = jnp.dot(block, w_gate, preferred_element_type=jnp.float32)
        value = jnp.dot(block, w_value, preferred_element_type=jnp.float32)
        act = (jax.nn.silu(gate) * value).astype(jnp.bfloat16)
        return jnp.dot(act, w_out, preferred_element_type=jnp.float32).astype(jnp.bfloat16)
    return lax.map(one_block, blocks).reshape(conv_out.shape)

def stream_layer(states, bases, embed_table, conv_kernel, conv_bias, norm_gain, w_gate, w_value, w_out):
    values = states.astype(jnp.float32) + embed_table.astype(jnp.float32)[bases]
    normed = rms_normed(values, norm_gain)
    conv_out = depthwise(normed, conv_kernel, conv_bias)
    return (values, pointwise(conv_out, w_gate, w_value, w_out))

def reference(tokens, masked, hidden_forward, hidden_reverse, embed_table, conv_kernel, conv_bias, norm_gain, w_gate, w_value, w_out):
    base_in = jnp.where(masked == 1, 4, tokens).astype(jnp.int32)
    base_rc = jnp.where(masked == 1, 4, 3 - tokens).astype(jnp.int32)[:, ::-1]
    x_fwd, branch_fwd = stream_layer(hidden_forward, base_in, embed_table, conv_kernel, conv_bias, norm_gain, w_gate, w_value, w_out)
    x_rev, branch_rev = stream_layer(hidden_reverse, base_rc, embed_table, conv_kernel, conv_bias, norm_gain, w_gate, w_value, w_out)
    out_forward = x_fwd + branch_fwd.astype(jnp.float32) + branch_rev[:, ::-1, ::-1].astype(jnp.float32)
    out_reverse = x_rev + branch_rev.astype(jnp.float32) + branch_fwd[:, ::-1, ::-1].astype(jnp.float32)
    return (out_forward.astype(jnp.bfloat16), out_reverse.astype(jnp.bfloat16))
```

```python
import jax
import jax.numpy as jnp
from jax import lax
from jax.sharding import PartitionSpec as P


def mirror(value, axes, count):
    return lax.ppermute(value, axes, [(k, count - 1 - k) for k in range(count)])


def padded_2(cells, axis, dim, width):
    count = lax.axis_size(axis)
    ends = count - 1
    head = lax.slice_in_dim(cells, 0, width, axis=dim)
    tail = lax.slice_in_dim(cells, cells.shape[dim] - width, cells.shape[dim], axis=dim)
    return jnp.concatenate(
        [
            lax.ppermute(tail, axis, [(i, (i + 1) % count) for i in range(ends)]),
            cells,
            lax.ppermute(head, axis, [((i + 1) % count, i) for i in range(ends)]),
        ],
        axis=dim,
    )


def embedded(bases, table):
    out = jnp.zeros(bases.shape + (table.shape[1],), jnp.float32)
    for v in range(table.shape[0]):
        out = out + jnp.where(bases[..., None] == v, table[v], 0.0)
    return out


def local(
    tokens,
    masked,
    hidden_forward,
    hidden_reverse,
    embed_table,
    conv_kernel,
    conv_bias,
    norm_gain,
    w_gate,
    w_value,
    w_out,
):
    seq_count = lax.axis_size("seq")
    ch_count = lax.axis_size("ch")
    table = embed_table.astype(jnp.float32)
    base_in = jnp.where(masked == 1, 4, tokens)
    comp = jnp.where(masked == 1, 4, 3 - tokens)
    rev_here = jnp.flip(mirror(hidden_reverse, "seq", seq_count), axis=1)
    comp_back = jnp.flip(mirror(comp, "seq", seq_count), axis=1)

    x_fwd = hidden_forward.astype(jnp.float32) + embedded(base_in, table)
    x_rfp = rev_here.astype(jnp.float32) + embedded(comp, table)
    local_width = x_fwd.shape[-1]
    width = local_width * ch_count
    square_fwd, square_rev = lax.psum(
        (jnp.sum(x_fwd * x_fwd, axis=-1), jnp.sum(x_rfp * x_rfp, axis=-1)), "ch"
    )
    normed_fwd = (x_fwd * lax.rsqrt(square_fwd[..., None] / width + 1e-05) * norm_gain).astype(
        jnp.bfloat16
    )
    normed_rev = (x_rfp * lax.rsqrt(square_rev[..., None] / width + 1e-05) * norm_gain).astype(
        jnp.bfloat16
    )
    stacked = jnp.stack([normed_fwd, normed_rev])
    taps = conv_kernel.shape[0]
    half_width = taps // 2
    length = stacked.shape[2]
    padded = padded_2(stacked, "seq", 2, half_width).astype(jnp.float32)
    conv_f = jnp.zeros(normed_fwd.shape, jnp.float32) + conv_bias
    conv_r = jnp.zeros(normed_rev.shape, jnp.float32) + conv_bias
    for offset in range(taps):
        conv_f = conv_f + conv_kernel[offset] * padded[0, :, offset : offset + length]
        conv_r = conv_r + conv_kernel[taps - 1 - offset] * padded[1, :, offset : offset + length]
    conv_rows = jnp.concatenate([conv_f, conv_r]).astype(jnp.bfloat16).reshape(-1, local_width)
    piece = lax.all_gather(conv_rows, "ch", axis=1, tiled=True)
    gate = jnp.dot(piece, w_gate, preferred_element_type=jnp.float32)
    value = jnp.dot(piece, w_value, preferred_element_type=jnp.float32)
    act = (jax.nn.silu(gate) * value).astype(jnp.bfloat16)
    rows = act.shape[0] // 2
    act_pair = jnp.concatenate([act[:rows], act[rows:]], axis=1)
    w_pair = jnp.concatenate([w_out, jnp.flip(w_out, axis=1)], axis=0)
    shares = lax.psum_scatter(
        lax.dot_general(w_pair, act_pair, (((0,), (1,)), ((), ())), preferred_element_type=jnp.float32),
        "ch",
        scatter_dimension=0,
        tiled=True,
    )
    mixed = shares.T.reshape(x_fwd.shape)
    out_forward = x_fwd + mixed
    sent = mirror(mixed.astype(jnp.bfloat16), ("seq", "ch"), seq_count * ch_count)
    x_rev = hidden_reverse.astype(jnp.float32) + embedded(comp_back, table)
    out_reverse = x_rev + jnp.flip(sent, axis=(1, 2)).astype(jnp.float32)
    return (out_forward.astype(jnp.bfloat16), out_reverse.astype(jnp.bfloat16))


def solution(mesh):
    placed = (
        P(None, "seq"),
        P(None, "seq"),
        P(None, "seq", "ch"),
        P(None, "seq", "ch"),
        P(None, "ch"),
        P(None, "ch"),
        P("ch"),
        P("ch"),
        P(None, "ch"),
        P(None, "ch"),
        P("ch", None),
    )
    return jax.shard_map(
        local,
        mesh=mesh,
        in_specs=placed,
        out_specs=(P(None, "seq", "ch"), P(None, "seq", "ch")),
        check_vma=False,
    )
```

```python
import jax
import jax.numpy as jnp
from jax import lax
from jax.sharding import PartitionSpec as P


def mirror(value, axes, count):
    return lax.ppermute(value, axes, [(k, count - 1 - k) for k in range(count)])


def partner(value, axis, bit):
    mask = 1 << bit
    return lax.ppermute(value, axis, [(k, k ^ mask) for k in range(lax.axis_size(axis))])


def padded_2(cells, axis, dim, width):
    count = lax.axis_size(axis)
    ends = count - 1
    head = lax.slice_in_dim(cells, 0, width, axis=dim)
    tail = lax.slice_in_dim(cells, cells.shape[dim] - width, cells.shape[dim], axis=dim)
    return jnp.concatenate(
        [
            lax.ppermute(tail, axis, [(i, (i + 1) % count) for i in range(ends)]),
            cells,
            lax.ppermute(head, axis, [((i + 1) % count, i) for i in range(ends)]),
        ],
        axis=dim,
    )


def embedded(bases, table):
    out = jnp.zeros(bases.shape + (table.shape[1],), jnp.float32)
    for v in range(table.shape[0]):
        out = out + jnp.where(bases[..., None] == v, table[v], 0.0)
    return out


def gather_blocks(block, bits, me):
    cur = block[None]
    for bit in reversed(range(bits)):
        other = partner(cur, "ch", bit)
        low = ((me >> bit) & 1) == 0
        first = jnp.where(low, cur, other)
        second = jnp.where(low, other, cur)
        cur = jnp.stack([first, second], axis=1).reshape((-1,) + block.shape)
    return cur


def scatter_blocks(part, bits, me):
    cur = part
    for bit in range(bits):
        cur = cur.reshape((-1, 2) + part.shape[1:])
        low = ((me >> bit) & 1) == 0
        keep = jnp.where(low, cur[:, 0], cur[:, 1])
        give = jnp.where(low, cur[:, 1], cur[:, 0])
        if bit > 0:
            give = give.astype(jnp.bfloat16)
        cur = keep + partner(give, "ch", bit).astype(jnp.float32)
    return cur[0]


def local(
    tokens,
    masked,
    hidden_forward,
    hidden_reverse,
    embed_table,
    conv_kernel,
    conv_bias,
    norm_gain,
    w_gate,
    w_value,
    w_out,
):
    seq_count = lax.axis_size("seq")
    ch_count = lax.axis_size("ch")
    ch_bits = ch_count.bit_length() - 1
    me = lax.axis_index("ch")
    table = embed_table.astype(jnp.float32)
    base_in = jnp.where(masked == 1, 4, tokens)
    comp = jnp.where(masked == 1, 4, 3 - tokens)
    rev_here = jnp.flip(mirror(hidden_reverse, "seq", seq_count), axis=1)
    comp_back = jnp.flip(mirror(comp, "seq", seq_count), axis=1)

    local_width = hidden_forward.shape[-1]
    width = local_width * ch_count
    taps = conv_kernel.shape[0]
    half_width = taps // 2

    def conv_rows(hidden, bases, kernel):
        x = hidden.astype(jnp.float32) + embedded(bases, table)
        square = lax.psum(jnp.sum(x * x, axis=-1), "ch")
        normed = (x * lax.rsqrt(square[..., None] / width + 1e-05) * norm_gain).astype(jnp.bfloat16)
        length = normed.shape[1]
        padded = padded_2(normed, "seq", 1, half_width).astype(jnp.float32)
        conv = jnp.zeros(normed.shape, jnp.float32) + conv_bias
        for offset in range(taps):
            conv = conv + kernel[offset] * padded[:, offset : offset + length]
        return x, conv.astype(jnp.bfloat16).reshape(-1, local_width)

    def activation(rows):
        pieces = gather_blocks(rows, ch_bits, me)
        dims = (((0, 2), (0, 1)), ((), ()))
        gate = lax.dot_general(
            pieces, w_gate.reshape(ch_count, local_width, -1), dims, preferred_element_type=jnp.float32
        )
        value = lax.dot_general(
            pieces, w_value.reshape(ch_count, local_width, -1), dims, preferred_element_type=jnp.float32
        )
        return (jax.nn.silu(gate) * value).astype(jnp.bfloat16)

    x_fwd, rows_fwd = conv_rows(hidden_forward, base_in, conv_kernel)
    _, rows_rev = conv_rows(rev_here, comp, conv_kernel[::-1])
    act_fwd = activation(rows_fwd)
    act_rev = activation(rows_rev)
    contract = (((0,), (1,)), ((), ()))
    part = lax.dot_general(w_out, act_fwd, contract, preferred_element_type=jnp.float32) + jnp.flip(
        lax.dot_general(w_out, act_rev, contract, preferred_element_type=jnp.float32), axis=0
    )
    share = scatter_blocks(part.reshape(ch_count, local_width, -1), ch_bits, me)
    out_forward = x_fwd + share.T.reshape(x_fwd.shape)
    sent = mirror(
        jnp.flip(share, axis=0).T.astype(jnp.bfloat16).reshape(x_fwd.shape), ("seq", "ch"), seq_count * ch_count
    )
    x_rev = hidden_reverse.astype(jnp.float32) + embedded(comp_back, table)
    out_reverse = x_rev + jnp.flip(sent, axis=1).astype(jnp.float32)
    return (out_forward.astype(jnp.bfloat16), out_reverse.astype(jnp.bfloat16))


def solution(mesh):
    placed = (
        P(None, "seq"),
        P(None, "seq"),
        P(None, "seq", "ch"),
        P(None, "seq", "ch"),
        P(None, "ch"),
        P(None, "ch"),
        P("ch"),
        P("ch"),
        P(None, "ch"),
        P(None, "ch"),
        P("ch", None),
    )
    return jax.shard_map(
        local,
        mesh=mesh,
        in_specs=placed,
        out_specs=(P(None, "seq", "ch"), P(None, "seq", "ch")),
        check_vma=False,
    )
```

```python
import jax
import jax.numpy as jnp
from jax import lax
from jax.sharding import PartitionSpec as P


def mirror(value, axes, count):
    return lax.ppermute(value, axes, [(k, count - 1 - k) for k in range(count)])


def partner(value, axis, bit):
    mask = 1 << bit
    return lax.ppermute(value, axis, [(k, k ^ mask) for k in range(lax.axis_size(axis))])


def padded_2(cells, axis, dim, width):
    count = lax.axis_size(axis)
    ends = count - 1
    head = lax.slice_in_dim(cells, 0, width, axis=dim)
    tail = lax.slice_in_dim(cells, cells.shape[dim] - width, cells.shape[dim], axis=dim)
    return jnp.concatenate(
        [
            lax.ppermute(tail, axis, [(i, (i + 1) % count) for i in range(ends)]),
            cells,
            lax.ppermute(head, axis, [((i + 1) % count, i) for i in range(ends)]),
        ],
        axis=dim,
    )


def embedded(bases, table):
    out = jnp.zeros(bases.shape + (table.shape[1],), jnp.float32)
    for v in range(table.shape[0]):
        out = out + jnp.where(bases[..., None] == v, table[v], 0.0)
    return out


def gather_blocks(block, bits, me):
    cur = block[None]
    for bit in reversed(range(bits)):
        other = partner(cur, "ch", bit)
        low = ((me >> bit) & 1) == 0
        first = jnp.where(low, cur, other)
        second = jnp.where(low, other, cur)
        cur = jnp.stack([first, second], axis=1).reshape((-1,) + block.shape)
    return cur


def scatter_blocks(part, bits, me):
    cur = part
    rows, _, w = part.shape
    for bit in range(bits):
        cur = cur.reshape(rows, -1, 2, w)
        low = ((me >> bit) & 1) == 0
        keep = jnp.where(low, cur[:, :, 0], cur[:, :, 1])
        give = jnp.where(low, cur[:, :, 1], cur[:, :, 0])
        if bit > 0:
            give = give.astype(jnp.bfloat16)
        cur = keep + partner(give, "ch", bit).astype(jnp.float32)
    return cur[:, 0]


def reversal(n, block):
    rows = lax.broadcasted_iota(jnp.int32, (n, n), 0)
    cols = lax.broadcasted_iota(jnp.int32, (n, n), 1)
    same = rows // block == cols // block
    return (same & (rows % block + cols % block == block - 1)).astype(jnp.bfloat16)


def local(
    tokens,
    masked,
    hidden_forward,
    hidden_reverse,
    embed_table,
    conv_kernel,
    conv_bias,
    norm_gain,
    w_gate,
    w_value,
    w_out,
):
    seq_count = lax.axis_size("seq")
    ch_count = lax.axis_size("ch")
    ch_bits = ch_count.bit_length() - 1
    me = lax.axis_index("ch")
    table = embed_table.astype(jnp.float32)
    base_in = jnp.where(masked == 1, 4, tokens)
    comp = jnp.where(masked == 1, 4, 3 - tokens)
    rev_here = jnp.flip(mirror(hidden_reverse, "seq", seq_count), axis=1)
    comp_back = jnp.flip(mirror(comp, "seq", seq_count), axis=1)

    local_width = hidden_forward.shape[-1]
    width = local_width * ch_count
    taps = conv_kernel.shape[0]
    half_width = taps // 2

    def conv_rows(hidden, bases, kernel):
        x = hidden.astype(jnp.float32) + embedded(bases, table)
        square = lax.psum(jnp.sum(x * x, axis=-1), "ch")
        normed = (x * lax.rsqrt(square[..., None] / width + 1e-05) * norm_gain).astype(jnp.bfloat16)
        length = normed.shape[1]
        padded = padded_2(normed, "seq", 1, half_width).astype(jnp.float32)
        conv = jnp.zeros(normed.shape, jnp.float32) + conv_bias
        for offset in range(taps):
            conv = conv + kernel[offset] * padded[:, offset : offset + length]
        return x, conv.astype(jnp.bfloat16).reshape(-1, local_width)

    def activation(rows):
        pieces = gather_blocks(rows, ch_bits, me)
        dims = (((0, 2), (0, 1)), ((), ()))
        gate = lax.dot_general(
            pieces, w_gate.reshape(ch_count, local_width, -1), dims, preferred_element_type=jnp.float32
        )
        value = lax.dot_general(
            pieces, w_value.reshape(ch_count, local_width, -1), dims, preferred_element_type=jnp.float32
        )
        return (jax.nn.silu(gate) * value).astype(jnp.bfloat16)

    x_fwd, rows_fwd = conv_rows(hidden_forward, base_in, conv_kernel)
    _, rows_rev = conv_rows(rev_here, comp, conv_kernel[::-1])
    act_fwd = activation(rows_fwd)
    act_rev = activation(rows_rev)
    lane_flip = reversal(local_width, local_width)
    blocks = w_out.reshape(w_out.shape[0], ch_count, local_width)
    w_flip = jnp.concatenate([blocks[:, k] for k in reversed(range(ch_count))], axis=1)
    w_flip = jnp.dot(
        w_flip.reshape(-1, local_width), lane_flip, preferred_element_type=jnp.float32
    ).astype(jnp.bfloat16).reshape(w_out.shape)
    part = jnp.dot(act_fwd, w_out, preferred_element_type=jnp.float32) + jnp.dot(
        act_rev, w_flip, preferred_element_type=jnp.float32
    )
    share = scatter_blocks(part.reshape(part.shape[0], ch_count, local_width), ch_bits, me)
    out_forward = x_fwd + share.reshape(x_fwd.shape)
    row_flip = reversal(share.shape[0], x_fwd.shape[1])
    turned = jnp.dot(share.astype(jnp.bfloat16), lane_flip, preferred_element_type=jnp.float32)
    turned = jnp.dot(row_flip, turned.astype(jnp.bfloat16), preferred_element_type=jnp.float32)
    sent = mirror(turned.astype(jnp.bfloat16).reshape(x_fwd.shape), ("seq", "ch"), seq_count * ch_count)
    x_rev = hidden_reverse.astype(jnp.float32) + embedded(comp_back, table)
    out_reverse = x_rev + sent.astype(jnp.float32)
    return (out_forward.astype(jnp.bfloat16), out_reverse.astype(jnp.bfloat16))


def solution(mesh):
    placed = (
        P(None, "seq"),
        P(None, "seq"),
        P(None, "seq", "ch"),
        P(None, "seq", "ch"),
        P(None, "ch"),
        P(None, "ch"),
        P("ch"),
        P("ch"),
        P(None, "ch"),
        P(None, "ch"),
        P("ch", None),
    )
    return jax.shard_map(
        local,
        mesh=mesh,
        in_specs=placed,
        out_specs=(P(None, "seq", "ch"), P(None, "seq", "ch")),
        check_vma=False,
    )
```

```python
import jax
import jax.numpy as jnp
from jax import lax
from jax.sharding import PartitionSpec as P


def mirror(value, axes, count):
    return lax.ppermute(value, axes, [(k, count - 1 - k) for k in range(count)])


def partner(value, axis, bit):
    mask = 1 << bit
    return lax.ppermute(value, axis, [(k, k ^ mask) for k in range(lax.axis_size(axis))])


def padded_2(cells, axis, dim, width):
    count = lax.axis_size(axis)
    ends = count - 1
    head = lax.slice_in_dim(cells, 0, width, axis=dim)
    tail = lax.slice_in_dim(cells, cells.shape[dim] - width, cells.shape[dim], axis=dim)
    return jnp.concatenate(
        [
            lax.ppermute(tail, axis, [(i, (i + 1) % count) for i in range(ends)]),
            cells,
            lax.ppermute(head, axis, [((i + 1) % count, i) for i in range(ends)]),
        ],
        axis=dim,
    )


def embedded(bases, table):
    out = jnp.zeros(bases.shape + (table.shape[1],), jnp.float32)
    for v in range(table.shape[0]):
        out = out + jnp.where(bases[..., None] == v, table[v], 0.0)
    return out


def gather_blocks(block, bits, me):
    cur = block[None]
    for bit in reversed(range(bits)):
        other = partner(cur, "ch", bit)
        low = ((me >> bit) & 1) == 0
        first = jnp.where(low, cur, other)
        second = jnp.where(low, other, cur)
        cur = jnp.stack([first, second], axis=1).reshape((-1,) + block.shape)
    return cur


def scatter_blocks(part, bits, me):
    cur = part
    rows, _, w = part.shape
    for bit in range(bits):
        cur = cur.reshape(rows, -1, 2, w)
        low = ((me >> bit) & 1) == 0
        keep = jnp.where(low, cur[:, :, 0], cur[:, :, 1])
        give = jnp.where(low, cur[:, :, 1], cur[:, :, 0])
        if bit > 0:
            give = give.astype(jnp.bfloat16)
        cur = keep + partner(give, "ch", bit).astype(jnp.float32)
    return cur[:, 0]


def reversal(n, block):
    rows = lax.broadcasted_iota(jnp.int32, (n, n), 0)
    cols = lax.broadcasted_iota(jnp.int32, (n, n), 1)
    same = rows // block == cols // block
    return (same & (rows % block + cols % block == block - 1)).astype(jnp.bfloat16)


def local(
    tokens,
    masked,
    hidden_forward,
    hidden_reverse,
    embed_table,
    conv_kernel,
    conv_bias,
    norm_gain,
    w_gate,
    w_value,
    w_out,
):
    seq_count = lax.axis_size("seq")
    ch_count = lax.axis_size("ch")
    ch_bits = ch_count.bit_length() - 1
    me = lax.axis_index("ch")
    table = embed_table.astype(jnp.float32)
    base_in = jnp.where(masked == 1, 4, tokens)
    comp = jnp.where(masked == 1, 4, 3 - tokens)
    arrived = mirror(hidden_reverse, "seq", seq_count)
    comp_back = jnp.flip(mirror(comp, "seq", seq_count), axis=1)
    x_rev = hidden_reverse.astype(jnp.float32) + embedded(comp_back, table)
    arrived, x_rev = lax.optimization_barrier((arrived, x_rev))
    span = arrived.shape[1]
    rows_all = arrived.shape[0] * span
    rev_here = jnp.dot(
        reversal(rows_all, span), arrived.reshape(rows_all, -1), preferred_element_type=jnp.float32
    ).astype(jnp.bfloat16).reshape(arrived.shape)

    local_width = hidden_forward.shape[-1]
    width = local_width * ch_count
    taps = conv_kernel.shape[0]
    half_width = taps // 2

    def conv_rows(hidden, bases, kernel):
        x = hidden.astype(jnp.float32) + embedded(bases, table)
        square = lax.psum(jnp.sum(x * x, axis=-1), "ch")
        normed = (x * lax.rsqrt(square[..., None] / width + 1e-05) * norm_gain).astype(jnp.bfloat16)
        length = normed.shape[1]
        padded = padded_2(normed, "seq", 1, half_width).astype(jnp.float32)
        conv = jnp.zeros(normed.shape, jnp.float32) + conv_bias
        for offset in range(taps):
            conv = conv + kernel[offset] * padded[:, offset : offset + length]
        return x, conv.astype(jnp.bfloat16).reshape(-1, local_width)

    def activation(rows):
        pieces = gather_blocks(rows, ch_bits, me)
        dims = (((0, 2), (0, 1)), ((), ()))
        gate = lax.dot_general(
            pieces, w_gate.reshape(ch_count, local_width, -1), dims, preferred_element_type=jnp.float32
        )
        value = lax.dot_general(
            pieces, w_value.reshape(ch_count, local_width, -1), dims, preferred_element_type=jnp.float32
        )
        return (jax.nn.silu(gate) * value).astype(jnp.bfloat16)

    x_fwd, rows_fwd = conv_rows(hidden_forward, base_in, conv_kernel)
    _, rows_rev = conv_rows(rev_here, comp, conv_kernel[::-1])
    act_fwd = activation(rows_fwd)
    act_rev = activation(rows_rev)
    lane_flip = reversal(local_width, local_width)
    w_flip = jnp.dot(w_out, reversal(width, width), preferred_element_type=jnp.float32).astype(jnp.bfloat16)
    part = jnp.dot(act_fwd, w_out, preferred_element_type=jnp.float32) + jnp.dot(
        act_rev, w_flip, preferred_element_type=jnp.float32
    )
    share = scatter_blocks(part.reshape(part.shape[0], ch_count, local_width), ch_bits, me)
    out_forward = x_fwd + share.reshape(x_fwd.shape)
    row_flip = reversal(share.shape[0], x_fwd.shape[1])
    turned = jnp.dot(share.astype(jnp.bfloat16), lane_flip, preferred_element_type=jnp.float32)
    turned = jnp.dot(row_flip, turned.astype(jnp.bfloat16), preferred_element_type=jnp.float32)
    sent = mirror(turned.astype(jnp.bfloat16).reshape(x_fwd.shape), ("seq", "ch"), seq_count * ch_count)
    out_reverse = x_rev + sent.astype(jnp.float32)
    return (out_forward.astype(jnp.bfloat16), out_reverse.astype(jnp.bfloat16))


def solution(mesh):
    placed = (
        P(None, "seq"),
        P(None, "seq"),
        P(None, "seq", "ch"),
        P(None, "seq", "ch"),
        P(None, "ch"),
        P(None, "ch"),
        P("ch"),
        P("ch"),
        P(None, "ch"),
        P(None, "ch"),
        P("ch", None),
    )
    return jax.shard_map(
        local,
        mesh=mesh,
        in_specs=placed,
        out_specs=(P(None, "seq", "ch"), P(None, "seq", "ch")),
        check_vma=False,
    )
```

```python
import jax
import jax.numpy as jnp
from jax import lax
from jax.sharding import PartitionSpec as P


def mirror(value, axes, count):
    return lax.ppermute(value, axes, [(k, count - 1 - k) for k in range(count)])


def partner(value, axis, bit):
    mask = 1 << bit
    return lax.ppermute(value, axis, [(k, k ^ mask) for k in range(lax.axis_size(axis))])


def padded_2(cells, axis, dim, width):
    count = lax.axis_size(axis)
    ends = count - 1
    head = lax.slice_in_dim(cells, 0, width, axis=dim)
    tail = lax.slice_in_dim(cells, cells.shape[dim] - width, cells.shape[dim], axis=dim)
    return jnp.concatenate(
        [
            lax.ppermute(tail, axis, [(i, (i + 1) % count) for i in range(ends)]),
            cells,
            lax.ppermute(head, axis, [((i + 1) % count, i) for i in range(ends)]),
        ],
        axis=dim,
    )


def embedded(bases, table):
    out = jnp.zeros(bases.shape + (table.shape[1],), jnp.float32)
    for v in range(table.shape[0]):
        out = out + jnp.where(bases[..., None] == v, table[v], 0.0)
    return out


def gather_blocks(block, bits, me):
    cur = block[None]
    for bit in reversed(range(bits)):
        other = partner(cur, "ch", bit)
        low = ((me >> bit) & 1) == 0
        first = jnp.where(low, cur, other)
        second = jnp.where(low, other, cur)
        cur = jnp.stack([first, second], axis=1).reshape((-1,) + block.shape)
    return cur


def scatter_blocks(part, bits, me):
    cur = part
    rows, _, w = part.shape
    for bit in range(bits):
        cur = cur.reshape(rows, -1, 2, w)
        low = ((me >> bit) & 1) == 0
        keep = jnp.where(low, cur[:, :, 0], cur[:, :, 1])
        give = jnp.where(low, cur[:, :, 1], cur[:, :, 0])
        if bit > 0:
            give = give.astype(jnp.bfloat16)
        cur = keep + partner(give, "ch", bit).astype(jnp.float32)
    return cur[:, 0]


def reversal(n, block):
    rows = lax.broadcasted_iota(jnp.int32, (n, n), 0)
    cols = lax.broadcasted_iota(jnp.int32, (n, n), 1)
    same = rows // block == cols // block
    return (same & (rows % block + cols % block == block - 1)).astype(jnp.bfloat16)


def chain(
    tokens,
    masked,
    hidden_forward,
    hidden_reverse,
    table,
    conv_kernel,
    conv_bias,
    norm_gain,
    w_gate,
    w_value,
    w_out,
    w_flip,
    after,
):
    seq_count = lax.axis_size("seq")
    ch_count = lax.axis_size("ch")
    ch_bits = ch_count.bit_length() - 1
    me = lax.axis_index("ch")
    base_in = jnp.where(masked == 1, 4, tokens)
    comp = jnp.where(masked == 1, 4, 3 - tokens)
    arrived = mirror(hidden_reverse, "seq", seq_count)
    comp_back = jnp.flip(mirror(comp, "seq", seq_count), axis=1)
    x_rev = hidden_reverse.astype(jnp.float32) + embedded(comp_back, table)
    arrived, x_rev = lax.optimization_barrier((arrived, x_rev))
    span = arrived.shape[1]
    rows_all = arrived.shape[0] * span
    rev_here = jnp.dot(
        reversal(rows_all, span), arrived.reshape(rows_all, -1), preferred_element_type=jnp.float32
    ).astype(jnp.bfloat16).reshape(arrived.shape)

    local_width = hidden_forward.shape[-1]
    width = local_width * ch_count
    taps = conv_kernel.shape[0]
    half_width = taps // 2

    def conv_rows(hidden, bases, kernel):
        x = hidden.astype(jnp.float32) + embedded(bases, table)
        own = jnp.sum(x * x, axis=-1)
        if after is not None:
            own, _ = lax.optimization_barrier((own, after))
        square = lax.psum(own, "ch")
        normed = (x * lax.rsqrt(square[..., None] / width + 1e-05) * norm_gain).astype(jnp.bfloat16)
        length = normed.shape[1]
        padded = padded_2(normed, "seq", 1, half_width).astype(jnp.float32)
        conv = jnp.zeros(normed.shape, jnp.float32) + conv_bias
        for offset in range(taps):
            conv = conv + kernel[offset] * padded[:, offset : offset + length]
        return x, conv.astype(jnp.bfloat16).reshape(-1, local_width), square

    def activation(rows):
        pieces = gather_blocks(rows, ch_bits, me)
        dims = (((0, 2), (0, 1)), ((), ()))
        gate = lax.dot_general(
            pieces, w_gate.reshape(ch_count, local_width, -1), dims, preferred_element_type=jnp.float32
        )
        value = lax.dot_general(
            pieces, w_value.reshape(ch_count, local_width, -1), dims, preferred_element_type=jnp.float32
        )
        return (jax.nn.silu(gate) * value).astype(jnp.bfloat16)

    x_fwd, rows_fwd, square = conv_rows(hidden_forward, base_in, conv_kernel)
    _, rows_rev, square_rev = conv_rows(rev_here, comp, conv_kernel[::-1])
    act_fwd = activation(rows_fwd)
    act_rev = activation(rows_rev)
    part = jnp.dot(act_fwd, w_out, preferred_element_type=jnp.float32) + jnp.dot(
        act_rev, w_flip, preferred_element_type=jnp.float32
    )
    share = scatter_blocks(part.reshape(part.shape[0], ch_count, local_width), ch_bits, me)
    out_forward = x_fwd + share.reshape(x_fwd.shape)
    row_flip = reversal(share.shape[0], x_fwd.shape[1])
    turned = jnp.dot(share.astype(jnp.bfloat16), reversal(local_width, local_width), preferred_element_type=jnp.float32)
    turned = jnp.dot(row_flip, turned.astype(jnp.bfloat16), preferred_element_type=jnp.float32)
    sent = mirror(turned.astype(jnp.bfloat16).reshape(x_fwd.shape), ("seq", "ch"), seq_count * ch_count)
    out_reverse = x_rev + sent.astype(jnp.float32)
    return (out_forward.astype(jnp.bfloat16), out_reverse.astype(jnp.bfloat16)), (square, square_rev)


def local(
    tokens,
    masked,
    hidden_forward,
    hidden_reverse,
    embed_table,
    conv_kernel,
    conv_bias,
    norm_gain,
    w_gate,
    w_value,
    w_out,
):
    width = w_out.shape[1]
    table = embed_table.astype(jnp.float32)
    w_flip = jnp.dot(w_out, reversal(width, width), preferred_element_type=jnp.float32).astype(jnp.bfloat16)
    outs = []
    after = None
    for s in range(tokens.shape[0]):
        pick = slice(s, s + 1)
        out, after = chain(
            tokens[pick],
            masked[pick],
            hidden_forward[pick],
            hidden_reverse[pick],
            table,
            conv_kernel,
            conv_bias,
            norm_gain,
            w_gate,
            w_value,
            w_out,
            w_flip,
            after,
        )
        outs.append(out)
    return tuple(jnp.concatenate([o[k] for o in outs]) for k in range(2))


def solution(mesh):
    placed = (
        P(None, "seq"),
        P(None, "seq"),
        P(None, "seq", "ch"),
        P(None, "seq", "ch"),
        P(None, "ch"),
        P(None, "ch"),
        P("ch"),
        P("ch"),
        P(None, "ch"),
        P(None, "ch"),
        P("ch", None),
    )
    return jax.shard_map(
        local,
        mesh=mesh,
        in_specs=placed,
        out_specs=(P(None, "seq", "ch"), P(None, "seq", "ch")),
        check_vma=False,
    )
```

```python
import jax
import jax.numpy as jnp
from jax import lax
from jax.sharding import PartitionSpec as P


def mirror(value, axes, count):
    return lax.ppermute(value, axes, [(k, count - 1 - k) for k in range(count)])


def partner(value, axis, bit):
    mask = 1 << bit
    return lax.ppermute(value, axis, [(k, k ^ mask) for k in range(lax.axis_size(axis))])


def padded_2(cells, axis, dim, width):
    count = lax.axis_size(axis)
    ends = count - 1
    head = lax.slice_in_dim(cells, 0, width, axis=dim)
    tail = lax.slice_in_dim(cells, cells.shape[dim] - width, cells.shape[dim], axis=dim)
    return jnp.concatenate(
        [
            lax.ppermute(tail, axis, [(i, (i + 1) % count) for i in range(ends)]),
            cells,
            lax.ppermute(head, axis, [((i + 1) % count, i) for i in range(ends)]),
        ],
        axis=dim,
    )


def embedded(bases, table):
    out = jnp.zeros(bases.shape + (table.shape[1],), jnp.float32)
    for v in range(table.shape[0]):
        out = out + jnp.where(bases[..., None] == v, table[v], 0.0)
    return out


def gather_blocks(block, bits, me):
    cur = block[None]
    for bit in reversed(range(bits)):
        other = partner(cur, "ch", bit)
        low = ((me >> bit) & 1) == 0
        first = jnp.where(low, cur, other)
        second = jnp.where(low, other, cur)
        cur = jnp.stack([first, second], axis=1).reshape((-1,) + block.shape)
    return cur


def scatter_blocks(part, bits, me):
    cur = part
    rows, _, w = part.shape
    for bit in range(bits):
        cur = cur.reshape(rows, -1, 2, w)
        low = ((me >> bit) & 1) == 0
        keep = jnp.where(low, cur[:, :, 0], cur[:, :, 1])
        give = jnp.where(low, cur[:, :, 1], cur[:, :, 0])
        if bit > 0:
            give = give.astype(jnp.bfloat16)
        cur = keep + partner(give, "ch", bit).astype(jnp.float32)
    return cur[:, 0]


def reversal(n, block):
    rows = lax.broadcasted_iota(jnp.int32, (n, n), 0)
    cols = lax.broadcasted_iota(jnp.int32, (n, n), 1)
    same = rows // block == cols // block
    return (same & (rows % block + cols % block == block - 1)).astype(jnp.bfloat16)


def local(
    tokens,
    masked,
    hidden_forward,
    hidden_reverse,
    embed_table,
    conv_kernel,
    conv_bias,
    norm_gain,
    w_gate,
    w_value,
    w_out,
):
    seq_count = lax.axis_size("seq")
    ch_count = lax.axis_size("ch")
    ch_bits = ch_count.bit_length() - 1
    me = lax.axis_index("ch")
    table = embed_table.astype(jnp.float32)
    base_in = jnp.where(masked == 1, 4, tokens)
    comp = jnp.where(masked == 1, 4, 3 - tokens)
    arrived = mirror(hidden_reverse, "seq", seq_count)
    comp_back = jnp.flip(mirror(comp, "seq", seq_count), axis=1)
    x_rev = hidden_reverse.astype(jnp.float32) + embedded(comp_back, table)
    arrived, x_rev = lax.optimization_barrier((arrived, x_rev))
    span = arrived.shape[1]
    rows_all = arrived.shape[0] * span
    rev_here = jnp.dot(
        reversal(rows_all, span), arrived.reshape(rows_all, -1), preferred_element_type=jnp.float32
    ).astype(jnp.bfloat16).reshape(arrived.shape)

    local_width = hidden_forward.shape[-1]
    width = local_width * ch_count
    taps = conv_kernel.shape[0]
    half_width = taps // 2

    x_fwd = hidden_forward.astype(jnp.float32) + embedded(base_in, table)
    x_rfp = rev_here.astype(jnp.float32) + embedded(comp, table)
    square_fwd, square_rev = lax.psum(
        (jnp.sum(x_fwd * x_fwd, axis=-1), jnp.sum(x_rfp * x_rfp, axis=-1)), "ch"
    )
    normed_fwd = (x_fwd * lax.rsqrt(square_fwd[..., None] / width + 1e-05) * norm_gain).astype(
        jnp.bfloat16
    )
    normed_rev = (x_rfp * lax.rsqrt(square_rev[..., None] / width + 1e-05) * norm_gain).astype(
        jnp.bfloat16
    )
    stacked = jnp.stack([normed_fwd, normed_rev])
    length = stacked.shape[2]
    padded = padded_2(stacked, "seq", 2, half_width).astype(jnp.float32)
    conv_f = jnp.zeros(normed_fwd.shape, jnp.float32) + conv_bias
    conv_r = jnp.zeros(normed_rev.shape, jnp.float32) + conv_bias
    for offset in range(taps):
        conv_f = conv_f + conv_kernel[offset] * padded[0, :, offset : offset + length]
        conv_r = conv_r + conv_kernel[taps - 1 - offset] * padded[1, :, offset : offset + length]
    rows = jnp.concatenate([conv_f, conv_r]).astype(jnp.bfloat16).reshape(-1, local_width)
    pieces = gather_blocks(rows, ch_bits, me)
    dims = (((0, 2), (0, 1)), ((), ()))
    gate = lax.dot_general(
        pieces, w_gate.reshape(ch_count, local_width, -1), dims, preferred_element_type=jnp.float32
    )
    value = lax.dot_general(
        pieces, w_value.reshape(ch_count, local_width, -1), dims, preferred_element_type=jnp.float32
    )
    act = (jax.nn.silu(gate) * value).astype(jnp.bfloat16)
    half = act.shape[0] // 2
    act_fwd = act[:half]
    act_rev = act[half:]
    lane_flip = reversal(local_width, local_width)
    w_flip = jnp.dot(w_out, reversal(width, width), preferred_element_type=jnp.float32).astype(jnp.bfloat16)
    part = jnp.dot(act_fwd, w_out, preferred_element_type=jnp.float32) + jnp.dot(
        act_rev, w_flip, preferred_element_type=jnp.float32
    )
    share = scatter_blocks(part.reshape(part.shape[0], ch_count, local_width), ch_bits, me)
    out_forward = x_fwd + share.reshape(x_fwd.shape)
    row_flip = reversal(share.shape[0], x_fwd.shape[1])
    turned = jnp.dot(share.astype(jnp.bfloat16), lane_flip, preferred_element_type=jnp.float32)
    turned = jnp.dot(row_flip, turned.astype(jnp.bfloat16), preferred_element_type=jnp.float32)
    sent = mirror(turned.astype(jnp.bfloat16).reshape(x_fwd.shape), ("seq", "ch"), seq_count * ch_count)
    out_reverse = x_rev + sent.astype(jnp.float32)
    return (out_forward.astype(jnp.bfloat16), out_reverse.astype(jnp.bfloat16))


def solution(mesh):
    placed = (
        P(None, "seq"),
        P(None, "seq"),
        P(None, "seq", "ch"),
        P(None, "seq", "ch"),
        P(None, "ch"),
        P(None, "ch"),
        P("ch"),
        P("ch"),
        P(None, "ch"),
        P(None, "ch"),
        P("ch", None),
    )
    return jax.shard_map(
        local,
        mesh=mesh,
        in_specs=placed,
        out_specs=(P(None, "seq", "ch"), P(None, "seq", "ch")),
        check_vma=False,
    )
```

```python
import jax
import jax.numpy as jnp
from jax import lax
from jax.sharding import PartitionSpec as P


def mirror(value, axes, count):
    return lax.ppermute(value, axes, [(k, count - 1 - k) for k in range(count)])


def partner(value, axis, bit):
    mask = 1 << bit
    return lax.ppermute(value, axis, [(k, k ^ mask) for k in range(lax.axis_size(axis))])


def padded_2(cells, axis, dim, width):
    count = lax.axis_size(axis)
    ends = count - 1
    head = lax.slice_in_dim(cells, 0, width, axis=dim)
    tail = lax.slice_in_dim(cells, cells.shape[dim] - width, cells.shape[dim], axis=dim)
    return jnp.concatenate(
        [
            lax.ppermute(tail, axis, [(i, (i + 1) % count) for i in range(ends)]),
            cells,
            lax.ppermute(head, axis, [((i + 1) % count, i) for i in range(ends)]),
        ],
        axis=dim,
    )


def embedded(bases, table):
    onehot = (bases[..., None] == jnp.arange(table.shape[0], dtype=jnp.int32)).astype(table.dtype)
    return jnp.einsum("sbv,vc->sbc", onehot, table, preferred_element_type=jnp.float32)


def gather_blocks(block, bits, me):
    cur = block[None]
    for bit in reversed(range(bits)):
        other = partner(cur, "ch", bit)
        low = ((me >> bit) & 1) == 0
        first = jnp.where(low, cur, other)
        second = jnp.where(low, other, cur)
        cur = jnp.stack([first, second], axis=1).reshape((-1,) + block.shape)
    return cur


def scatter_blocks(part, bits, me):
    cur = part
    rows, _, w = part.shape
    for bit in range(bits):
        cur = cur.reshape(rows, -1, 2, w)
        low = ((me >> bit) & 1) == 0
        keep = jnp.where(low, cur[:, :, 0], cur[:, :, 1])
        give = jnp.where(low, cur[:, :, 1], cur[:, :, 0])
        if bit > 0:
            give = give.astype(jnp.bfloat16)
        cur = keep + partner(give, "ch", bit).astype(jnp.float32)
    return cur[:, 0]


def reversal(n, block):
    rows = lax.broadcasted_iota(jnp.int32, (n, n), 0)
    cols = lax.broadcasted_iota(jnp.int32, (n, n), 1)
    same = rows // block == cols // block
    return (same & (rows % block + cols % block == block - 1)).astype(jnp.bfloat16)


def local(
    tokens,
    masked,
    hidden_forward,
    hidden_reverse,
    embed_table,
    conv_kernel,
    conv_bias,
    norm_gain,
    w_gate,
    w_value,
    w_out,
):
    seq_count = lax.axis_size("seq")
    ch_count = lax.axis_size("ch")
    ch_bits = ch_count.bit_length() - 1
    me = lax.axis_index("ch")
    table = embed_table
    base_in = jnp.where(masked == 1, 4, tokens)
    comp = jnp.where(masked == 1, 4, 3 - tokens)
    arrived = mirror(hidden_reverse, "seq", seq_count)
    comp_back = jnp.flip(mirror(comp, "seq", seq_count), axis=1)
    x_rev = hidden_reverse.astype(jnp.float32) + embedded(comp_back, table)
    arrived, x_rev = lax.optimization_barrier((arrived, x_rev))
    span = arrived.shape[1]
    rows_all = arrived.shape[0] * span
    rev_here = jnp.dot(
        reversal(rows_all, span), arrived.reshape(rows_all, -1), preferred_element_type=jnp.float32
    ).astype(jnp.bfloat16).reshape(arrived.shape)

    local_width = hidden_forward.shape[-1]
    width = local_width * ch_count
    taps = conv_kernel.shape[0]
    half_width = taps // 2

    x_fwd = hidden_forward.astype(jnp.float32) + embedded(base_in, table)
    x_rfp = rev_here.astype(jnp.float32) + embedded(comp, table)
    square_fwd, square_rev = lax.psum(
        (jnp.sum(x_fwd * x_fwd, axis=-1), jnp.sum(x_rfp * x_rfp, axis=-1)), "ch"
    )
    normed_fwd = (x_fwd * lax.rsqrt(square_fwd[..., None] / width + 1e-05) * norm_gain).astype(
        jnp.bfloat16
    )
    normed_rev = (x_rfp * lax.rsqrt(square_rev[..., None] / width + 1e-05) * norm_gain).astype(
        jnp.bfloat16
    )
    stacked = jnp.stack([normed_fwd, normed_rev])
    length = stacked.shape[2]
    padded = padded_2(stacked, "seq", 2, half_width).astype(jnp.float32)
    conv_f = jnp.zeros(normed_fwd.shape, jnp.float32) + conv_bias
    conv_r = jnp.zeros(normed_rev.shape, jnp.float32) + conv_bias
    for offset in range(taps):
        conv_f = conv_f + conv_kernel[offset] * padded[0, :, offset : offset + length]
        conv_r = conv_r + conv_kernel[taps - 1 - offset] * padded[1, :, offset : offset + length]
    rows = jnp.concatenate([conv_f, conv_r]).astype(jnp.bfloat16).reshape(-1, local_width)
    pieces = gather_blocks(rows, ch_bits, me)
    dims = (((0, 2), (0, 1)), ((), ()))
    gate = lax.dot_general(
        pieces, w_gate.reshape(ch_count, local_width, -1), dims, preferred_element_type=jnp.float32
    )
    value = lax.dot_general(
        pieces, w_value.reshape(ch_count, local_width, -1), dims, preferred_element_type=jnp.float32
    )
    act = (jax.nn.silu(gate) * value).astype(jnp.bfloat16)
    half = act.shape[0] // 2
    act_fwd = act[:half]
    act_rev = act[half:]
    lane_flip = reversal(local_width, local_width)
    w_flip = jnp.dot(w_out, reversal(width, width), preferred_element_type=jnp.float32).astype(jnp.bfloat16)
    part = jnp.dot(act_fwd, w_out, preferred_element_type=jnp.float32) + jnp.dot(
        act_rev, w_flip, preferred_element_type=jnp.float32
    )
    share = scatter_blocks(part.reshape(part.shape[0], ch_count, local_width), ch_bits, me)
    out_forward = x_fwd + share.reshape(x_fwd.shape)
    row_flip = reversal(share.shape[0], x_fwd.shape[1])
    turned = jnp.dot(share.astype(jnp.bfloat16), lane_flip, preferred_element_type=jnp.float32)
    turned = jnp.dot(row_flip, turned.astype(jnp.bfloat16), preferred_element_type=jnp.float32)
    sent = mirror(turned.astype(jnp.bfloat16).reshape(x_fwd.shape), ("seq", "ch"), seq_count * ch_count)
    out_reverse = x_rev + sent.astype(jnp.float32)
    return (out_forward.astype(jnp.bfloat16), out_reverse.astype(jnp.bfloat16))


def solution(mesh):
    placed = (
        P(None, "seq"),
        P(None, "seq"),
        P(None, "seq", "ch"),
        P(None, "seq", "ch"),
        P(None, "ch"),
        P(None, "ch"),
        P("ch"),
        P("ch"),
        P(None, "ch"),
        P(None, "ch"),
        P("ch", None),
    )
    return jax.shard_map(
        local,
        mesh=mesh,
        in_specs=placed,
        out_specs=(P(None, "seq", "ch"), P(None, "seq", "ch")),
        check_vma=False,
    )
```

```python
import jax
import jax.numpy as jnp
from jax import lax
from jax.sharding import PartitionSpec as P


def mirror(value, axes, count):
    return lax.ppermute(value, axes, [(k, count - 1 - k) for k in range(count)])


def partner(value, axis, bit):
    mask = 1 << bit
    return lax.ppermute(value, axis, [(k, k ^ mask) for k in range(lax.axis_size(axis))])


def padded_2(cells, axis, dim, width):
    count = lax.axis_size(axis)
    ends = count - 1
    head = lax.slice_in_dim(cells, 0, width, axis=dim)
    tail = lax.slice_in_dim(cells, cells.shape[dim] - width, cells.shape[dim], axis=dim)
    return jnp.concatenate(
        [
            lax.ppermute(tail, axis, [(i, (i + 1) % count) for i in range(ends)]),
            cells,
            lax.ppermute(head, axis, [((i + 1) % count, i) for i in range(ends)]),
        ],
        axis=dim,
    )


def embedded(bases, table):
    out = jnp.zeros(bases.shape + (table.shape[1],), jnp.float32)
    for v in range(table.shape[0]):
        out = out + jnp.where(bases[..., None] == v, table[v], 0.0)
    return out


def gather_blocks(block, bits, me):
    cur = block[None]
    for bit in reversed(range(bits)):
        other = partner(cur, "ch", bit)
        low = ((me >> bit) & 1) == 0
        first = jnp.where(low, cur, other)
        second = jnp.where(low, other, cur)
        cur = jnp.stack([first, second], axis=1).reshape((-1,) + block.shape)
    return cur


def scatter_blocks(part, bits, me):
    cur = part
    rows, _, w = part.shape
    for bit in range(bits):
        cur = cur.reshape(rows, -1, 2, w)
        low = ((me >> bit) & 1) == 0
        keep = jnp.where(low, cur[:, :, 0], cur[:, :, 1])
        give = jnp.where(low, cur[:, :, 1], cur[:, :, 0])
        if bit > 0:
            give = give.astype(jnp.bfloat16)
        cur = keep + partner(give, "ch", bit).astype(jnp.float32)
    return cur[:, 0]


def reversal(n, block):
    rows = lax.broadcasted_iota(jnp.int32, (n, n), 0)
    cols = lax.broadcasted_iota(jnp.int32, (n, n), 1)
    same = rows // block == cols // block
    return (same & (rows % block + cols % block == block - 1)).astype(jnp.bfloat16)


def local(
    tokens,
    masked,
    hidden_forward,
    hidden_reverse,
    embed_table,
    conv_kernel,
    conv_bias,
    norm_gain,
    w_gate,
    w_value,
    w_out,
):
    seq_count = lax.axis_size("seq")
    ch_count = lax.axis_size("ch")
    ch_bits = ch_count.bit_length() - 1
    me = lax.axis_index("ch")
    table = embed_table.astype(jnp.float32)
    base_in = jnp.where(masked == 1, 4, tokens)
    comp = jnp.where(masked == 1, 4, 3 - tokens)
    arrived = mirror(hidden_reverse, "seq", seq_count)
    comp_back = jnp.flip(mirror(comp, "seq", seq_count), axis=1)
    x_rev = hidden_reverse.astype(jnp.float32) + embedded(comp_back, table)
    arrived, x_rev = lax.optimization_barrier((arrived, x_rev))
    span = arrived.shape[1]
    rows_all = arrived.shape[0] * span
    rev_here = jnp.dot(
        reversal(rows_all, span), arrived.reshape(rows_all, -1), preferred_element_type=jnp.float32
    ).astype(jnp.bfloat16).reshape(arrived.shape)

    local_width = hidden_forward.shape[-1]
    width = local_width * ch_count
    taps = conv_kernel.shape[0]
    half_width = taps // 2

    n = seq_count
    place = lax.axis_index("seq")
    code = tokens + 4 * masked
    up = [(k, k + 1) for k in range(n - 1)]
    down = [(k + 1, k) for k in range(n - 1)]
    left_f, left_code = lax.ppermute((hidden_forward[:, -half_width:], code[:, -half_width:]), "seq", up)
    right_f, right_code = lax.ppermute((hidden_forward[:, :half_width], code[:, :half_width]), "seq", down)
    left_r = lax.ppermute(hidden_reverse[:, :half_width], "seq", [(k, n - k) for k in range(1, n)])
    right_r = lax.ppermute(hidden_reverse[:, -half_width:], "seq", [(k, n - 2 - k) for k in range(n - 1)])
    edge_code = jnp.concatenate([left_code, right_code], axis=1)
    edge_masked = edge_code >= 4
    edge_f = jnp.concatenate([left_f, right_f], axis=1).astype(jnp.float32) + embedded(
        jnp.where(edge_masked, 4, edge_code), table
    )
    edge_r = jnp.concatenate([jnp.flip(left_r, axis=1), jnp.flip(right_r, axis=1)], axis=1).astype(
        jnp.float32
    ) + embedded(jnp.where(edge_masked, 4, 3 - edge_code), table)
    side = jnp.arange(2 * half_width) < half_width
    valid = jnp.where(side, place > 0, place < n - 1)[None, :, None]

    x_fwd = hidden_forward.astype(jnp.float32) + embedded(base_in, table)
    x_rfp = rev_here.astype(jnp.float32) + embedded(comp, table)
    square_fwd, square_rev, square_ef, square_er = lax.psum(
        (
            jnp.sum(x_fwd * x_fwd, axis=-1),
            jnp.sum(x_rfp * x_rfp, axis=-1),
            jnp.sum(edge_f * edge_f, axis=-1),
            jnp.sum(edge_r * edge_r, axis=-1),
        ),
        "ch",
    )

    def normed(x, square):
        return (x * lax.rsqrt(square[..., None] / width + 1e-05) * norm_gain).astype(jnp.bfloat16)

    normed_fwd = normed(x_fwd, square_fwd)
    normed_rev = normed(x_rfp, square_rev)
    edges = jnp.where(valid, jnp.stack([normed(edge_f, square_ef), normed(edge_r, square_er)]), 0)
    stacked = jnp.stack([normed_fwd, normed_rev])
    length = stacked.shape[2]
    padded = jnp.concatenate(
        [edges[:, :, :half_width], stacked, edges[:, :, half_width:]], axis=2
    ).astype(jnp.float32)
    conv_f = jnp.zeros(normed_fwd.shape, jnp.float32) + conv_bias
    conv_r = jnp.zeros(normed_rev.shape, jnp.float32) + conv_bias
    for offset in range(taps):
        conv_f = conv_f + conv_kernel[offset] * padded[0, :, offset : offset + length]
        conv_r = conv_r + conv_kernel[taps - 1 - offset] * padded[1, :, offset : offset + length]
    rows = jnp.concatenate([conv_f, conv_r]).astype(jnp.bfloat16).reshape(-1, local_width)
    pieces = gather_blocks(rows, ch_bits, me)
    dims = (((0, 2), (0, 1)), ((), ()))
    gate = lax.dot_general(
        pieces, w_gate.reshape(ch_count, local_width, -1), dims, preferred_element_type=jnp.float32
    )
    value = lax.dot_general(
        pieces, w_value.reshape(ch_count, local_width, -1), dims, preferred_element_type=jnp.float32
    )
    act = (jax.nn.silu(gate) * value).astype(jnp.bfloat16)
    half = act.shape[0] // 2
    act_fwd = act[:half]
    act_rev = act[half:]
    lane_flip = reversal(local_width, local_width)
    w_flip = jnp.dot(w_out, reversal(width, width), preferred_element_type=jnp.float32).astype(jnp.bfloat16)
    part = jnp.dot(act_fwd, w_out, preferred_element_type=jnp.float32) + jnp.dot(
        act_rev, w_flip, preferred_element_type=jnp.float32
    )
    share = scatter_blocks(part.reshape(part.shape[0], ch_count, local_width), ch_bits, me)
    out_forward = x_fwd + share.reshape(x_fwd.shape)
    row_flip = reversal(share.shape[0], x_fwd.shape[1])
    turned = jnp.dot(share.astype(jnp.bfloat16), lane_flip, preferred_element_type=jnp.float32)
    turned = jnp.dot(row_flip, turned.astype(jnp.bfloat16), preferred_element_type=jnp.float32)
    sent = mirror(turned.astype(jnp.bfloat16).reshape(x_fwd.shape), ("seq", "ch"), seq_count * ch_count)
    out_reverse = x_rev + sent.astype(jnp.float32)
    return (out_forward.astype(jnp.bfloat16), out_reverse.astype(jnp.bfloat16))


def solution(mesh):
    placed = (
        P(None, "seq"),
        P(None, "seq"),
        P(None, "seq", "ch"),
        P(None, "seq", "ch"),
        P(None, "ch"),
        P(None, "ch"),
        P("ch"),
        P("ch"),
        P(None, "ch"),
        P(None, "ch"),
        P("ch", None),
    )
    return jax.shard_map(
        local,
        mesh=mesh,
        in_specs=placed,
        out_specs=(P(None, "seq", "ch"), P(None, "seq", "ch")),
        check_vma=False,
    )
```

```python
import jax
import jax.numpy as jnp
from jax import lax
from jax.sharding import PartitionSpec as P


def mirror(value, axes, count):
    return lax.ppermute(value, axes, [(k, count - 1 - k) for k in range(count)])


def partner(value, axis, bit):
    mask = 1 << bit
    return lax.ppermute(value, axis, [(k, k ^ mask) for k in range(lax.axis_size(axis))])


def padded_2(cells, axis, dim, width):
    count = lax.axis_size(axis)
    ends = count - 1
    head = lax.slice_in_dim(cells, 0, width, axis=dim)
    tail = lax.slice_in_dim(cells, cells.shape[dim] - width, cells.shape[dim], axis=dim)
    return jnp.concatenate(
        [
            lax.ppermute(tail, axis, [(i, (i + 1) % count) for i in range(ends)]),
            cells,
            lax.ppermute(head, axis, [((i + 1) % count, i) for i in range(ends)]),
        ],
        axis=dim,
    )


def embedded(bases, table):
    out = jnp.zeros(bases.shape + (table.shape[1],), jnp.float32)
    for v in range(table.shape[0]):
        out = out + jnp.where(bases[..., None] == v, table[v], 0.0)
    return out


def gather_blocks(block, bits, me):
    cur = block[None]
    for bit in reversed(range(bits)):
        other = partner(cur, "ch", bit)
        low = ((me >> bit) & 1) == 0
        first = jnp.where(low, cur, other)
        second = jnp.where(low, other, cur)
        cur = jnp.stack([first, second], axis=1).reshape((-1,) + block.shape)
    return cur


def scatter_blocks(part, bits, me):
    cur = part
    rows, _, w = part.shape
    for bit in range(bits):
        cur = cur.reshape(rows, -1, 2, w)
        low = ((me >> bit) & 1) == 0
        keep = jnp.where(low, cur[:, :, 0], cur[:, :, 1])
        give = jnp.where(low, cur[:, :, 1], cur[:, :, 0])
        cur = keep + partner(give.astype(jnp.bfloat16), "ch", bit).astype(jnp.float32)
    return cur[:, 0]


def reversal(n, block):
    rows = lax.broadcasted_iota(jnp.int32, (n, n), 0)
    cols = lax.broadcasted_iota(jnp.int32, (n, n), 1)
    same = rows // block == cols // block
    return (same & (rows % block + cols % block == block - 1)).astype(jnp.bfloat16)


def local(
    tokens,
    masked,
    hidden_forward,
    hidden_reverse,
    embed_table,
    conv_kernel,
    conv_bias,
    norm_gain,
    w_gate,
    w_value,
    w_out,
):
    seq_count = lax.axis_size("seq")
    ch_count = lax.axis_size("ch")
    ch_bits = ch_count.bit_length() - 1
    me = lax.axis_index("ch")
    table = embed_table.astype(jnp.float32)
    base_in = jnp.where(masked == 1, 4, tokens)
    comp = jnp.where(masked == 1, 4, 3 - tokens)
    span = hidden_reverse.shape[1]
    lanes = hidden_reverse.shape[2]
    if span % lanes == 0:
        extra = span // lanes
        packed = jnp.concatenate(
            [hidden_reverse, comp.astype(jnp.bfloat16).reshape(comp.shape[0], extra, lanes)], axis=1
        )
        packed = mirror(packed, "seq", seq_count)
        arrived = packed[:, :span]
        comp_back = jnp.flip(packed[:, span:].reshape(comp.shape).astype(jnp.int32), axis=1)
    else:
        arrived = mirror(hidden_reverse, "seq", seq_count)
        comp_back = jnp.flip(mirror(comp, "seq", seq_count), axis=1)
    x_rev = hidden_reverse.astype(jnp.float32) + embedded(comp_back, table)
    arrived, x_rev = lax.optimization_barrier((arrived, x_rev))
    span = arrived.shape[1]
    rows_all = arrived.shape[0] * span
    rev_here = jnp.dot(
        reversal(rows_all, span), arrived.reshape(rows_all, -1), preferred_element_type=jnp.float32
    ).astype(jnp.bfloat16).reshape(arrived.shape)

    local_width = hidden_forward.shape[-1]
    width = local_width * ch_count
    taps = conv_kernel.shape[0]
    half_width = taps // 2

    x_fwd = hidden_forward.astype(jnp.float32) + embedded(base_in, table)
    x_rfp = rev_here.astype(jnp.float32) + embedded(comp, table)
    square_fwd, square_rev = lax.psum(
        (jnp.sum(x_fwd * x_fwd, axis=-1), jnp.sum(x_rfp * x_rfp, axis=-1)), "ch"
    )
    normed_fwd = (x_fwd * lax.rsqrt(square_fwd[..., None] / width + 1e-05) * norm_gain).astype(
        jnp.bfloat16
    )
    normed_rev = (x_rfp * lax.rsqrt(square_rev[..., None] / width + 1e-05) * norm_gain).astype(
        jnp.bfloat16
    )
    stacked = jnp.stack([normed_fwd, normed_rev])
    length = stacked.shape[2]
    padded = padded_2(stacked, "seq", 2, half_width).astype(jnp.float32)
    conv_f = jnp.zeros(normed_fwd.shape, jnp.float32) + conv_bias
    conv_r = jnp.zeros(normed_rev.shape, jnp.float32) + conv_bias
    for offset in range(taps):
        conv_f = conv_f + conv_kernel[offset] * padded[0, :, offset : offset + length]
        conv_r = conv_r + conv_kernel[taps - 1 - offset] * padded[1, :, offset : offset + length]
    rows = jnp.concatenate([conv_f, conv_r]).astype(jnp.bfloat16).reshape(-1, local_width)
    pieces = gather_blocks(rows, ch_bits, me)
    dims = (((0, 2), (0, 1)), ((), ()))
    gate = lax.dot_general(
        pieces, w_gate.reshape(ch_count, local_width, -1), dims, preferred_element_type=jnp.float32
    )
    value = lax.dot_general(
        pieces, w_value.reshape(ch_count, local_width, -1), dims, preferred_element_type=jnp.float32
    )
    act = (jax.nn.silu(gate) * value).astype(jnp.bfloat16)
    half = act.shape[0] // 2
    act_fwd = act[:half]
    act_rev = act[half:]
    lane_flip = reversal(local_width, local_width)
    w_flip = jnp.dot(w_out, reversal(width, width), preferred_element_type=jnp.float32).astype(jnp.bfloat16)
    part = jnp.dot(act_fwd, w_out, preferred_element_type=jnp.float32) + jnp.dot(
        act_rev, w_flip, preferred_element_type=jnp.float32
    )
    share = scatter_blocks(part.reshape(part.shape[0], ch_count, local_width), ch_bits, me)
    out_forward = x_fwd + share.reshape(x_fwd.shape)
    row_flip = reversal(share.shape[0], x_fwd.shape[1])
    turned = jnp.dot(share.astype(jnp.bfloat16), lane_flip, preferred_element_type=jnp.float32)
    turned = jnp.dot(row_flip, turned.astype(jnp.bfloat16), preferred_element_type=jnp.float32)
    sent = mirror(turned.astype(jnp.bfloat16).reshape(x_fwd.shape), ("seq", "ch"), seq_count * ch_count)
    out_reverse = x_rev + sent.astype(jnp.float32)
    return (out_forward.astype(jnp.bfloat16), out_reverse.astype(jnp.bfloat16))


def solution(mesh):
    placed = (
        P(None, "seq"),
        P(None, "seq"),
        P(None, "seq", "ch"),
        P(None, "seq", "ch"),
        P(None, "ch"),
        P(None, "ch"),
        P("ch"),
        P("ch"),
        P(None, "ch"),
        P(None, "ch"),
        P("ch", None),
    )
    return jax.shard_map(
        local,
        mesh=mesh,
        in_specs=placed,
        out_specs=(P(None, "seq", "ch"), P(None, "seq", "ch")),
        check_vma=False,
    )
```

```python
import jax
import jax.numpy as jnp
from jax import lax
from jax.sharding import PartitionSpec as P


def mirror(value, axes, count):
    return lax.ppermute(value, axes, [(k, count - 1 - k) for k in range(count)])


def partner(value, axis, bit):
    mask = 1 << bit
    return lax.ppermute(value, axis, [(k, k ^ mask) for k in range(lax.axis_size(axis))])


def padded_2(cells, axis, dim, width):
    count = lax.axis_size(axis)
    ends = count - 1
    head = lax.slice_in_dim(cells, 0, width, axis=dim)
    tail = lax.slice_in_dim(cells, cells.shape[dim] - width, cells.shape[dim], axis=dim)
    return jnp.concatenate(
        [
            lax.ppermute(tail, axis, [(i, (i + 1) % count) for i in range(ends)]),
            cells,
            lax.ppermute(head, axis, [((i + 1) % count, i) for i in range(ends)]),
        ],
        axis=dim,
    )


def embedded(bases, table):
    out = jnp.zeros(bases.shape + (table.shape[1],), jnp.float32)
    for v in range(table.shape[0]):
        out = out + jnp.where(bases[..., None] == v, table[v], 0.0)
    return out


def gather_blocks(block, bits, me):
    cur = block[None]
    for bit in reversed(range(bits)):
        other = partner(cur, "ch", bit)
        low = ((me >> bit) & 1) == 0
        first = jnp.where(low, cur, other)
        second = jnp.where(low, other, cur)
        cur = jnp.stack([first, second], axis=1).reshape((-1,) + block.shape)
    return cur


def scatter_blocks(part, bits, me):
    cur = part
    rows, _, w = part.shape
    for bit in range(bits):
        cur = cur.reshape(rows, -1, 2, w)
        low = ((me >> bit) & 1) == 0
        keep = jnp.where(low, cur[:, :, 0], cur[:, :, 1])
        give = jnp.where(low, cur[:, :, 1], cur[:, :, 0])
        if bit > 0:
            give = give.astype(jnp.bfloat16)
        cur = keep + partner(give, "ch", bit).astype(jnp.float32)
    return cur[:, 0]


def reversal(n, block):
    rows = lax.broadcasted_iota(jnp.int32, (n, n), 0)
    cols = lax.broadcasted_iota(jnp.int32, (n, n), 1)
    same = rows // block == cols // block
    return (same & (rows % block + cols % block == block - 1)).astype(jnp.bfloat16)


def local(
    tokens,
    masked,
    hidden_forward,
    hidden_reverse,
    embed_table,
    conv_kernel,
    conv_bias,
    norm_gain,
    w_gate,
    w_value,
    w_out,
):
    seq_count = lax.axis_size("seq")
    ch_count = lax.axis_size("ch")
    ch_bits = ch_count.bit_length() - 1
    me = lax.axis_index("ch")
    table = embed_table.astype(jnp.float32)
    base_in = jnp.where(masked == 1, 4, tokens)
    comp = jnp.where(masked == 1, 4, 3 - tokens)
    comp_back = jnp.flip(mirror(comp, "seq", seq_count), axis=1)

    local_width = hidden_forward.shape[-1]
    width = local_width * ch_count
    taps = conv_kernel.shape[0]
    half_width = taps // 2

    x_fwd = hidden_forward.astype(jnp.float32) + embedded(base_in, table)
    x_rev = hidden_reverse.astype(jnp.float32) + embedded(comp_back, table)
    square_fwd, square_rev = lax.psum(
        (jnp.sum(x_fwd * x_fwd, axis=-1), jnp.sum(x_rev * x_rev, axis=-1)), "ch"
    )
    normed_fwd = (x_fwd * lax.rsqrt(square_fwd[..., None] / width + 1e-05) * norm_gain).astype(
        jnp.bfloat16
    )
    normed_rev = (x_rev * lax.rsqrt(square_rev[..., None] / width + 1e-05) * norm_gain).astype(
        jnp.bfloat16
    )
    stacked = jnp.stack([normed_fwd, normed_rev])
    length = stacked.shape[2]
    padded = padded_2(stacked, "seq", 2, half_width).astype(jnp.float32)
    conv = jnp.zeros(stacked.shape, jnp.float32) + conv_bias
    for offset in range(taps):
        conv = conv + conv_kernel[offset] * padded[:, :, offset : offset + length]
    conv = conv.astype(jnp.bfloat16)
    rows_fwd = conv[0].reshape(-1, local_width)
    rows_all = rows_fwd.shape[0]
    rows_rev = mirror(
        jnp.dot(
            reversal(rows_all, length), conv[1].reshape(rows_all, -1), preferred_element_type=jnp.float32
        ).astype(jnp.bfloat16),
        "seq",
        seq_count,
    )

    def activation(rows):
        pieces = gather_blocks(rows, ch_bits, me)
        dims = (((0, 2), (0, 1)), ((), ()))
        gate = lax.dot_general(
            pieces, w_gate.reshape(ch_count, local_width, -1), dims, preferred_element_type=jnp.float32
        )
        value = lax.dot_general(
            pieces, w_value.reshape(ch_count, local_width, -1), dims, preferred_element_type=jnp.float32
        )
        return (jax.nn.silu(gate) * value).astype(jnp.bfloat16)

    act_fwd = activation(rows_fwd)
    act_rev = activation(rows_rev)
    lane_flip = reversal(local_width, local_width)
    w_flip = jnp.dot(w_out, reversal(width, width), preferred_element_type=jnp.float32).astype(jnp.bfloat16)
    part = jnp.dot(act_fwd, w_out, preferred_element_type=jnp.float32) + jnp.dot(
        act_rev, w_flip, preferred_element_type=jnp.float32
    )
    share = scatter_blocks(part.reshape(part.shape[0], ch_count, local_width), ch_bits, me)
    out_forward = x_fwd + share.reshape(x_fwd.shape)
    row_flip = reversal(share.shape[0], x_fwd.shape[1])
    turned = jnp.dot(share.astype(jnp.bfloat16), lane_flip, preferred_element_type=jnp.float32)
    turned = jnp.dot(row_flip, turned.astype(jnp.bfloat16), preferred_element_type=jnp.float32)
    sent = mirror(turned.astype(jnp.bfloat16).reshape(x_fwd.shape), ("seq", "ch"), seq_count * ch_count)
    out_reverse = x_rev + sent.astype(jnp.float32)
    return (out_forward.astype(jnp.bfloat16), out_reverse.astype(jnp.bfloat16))


def solution(mesh):
    placed = (
        P(None, "seq"),
        P(None, "seq"),
        P(None, "seq", "ch"),
        P(None, "seq", "ch"),
        P(None, "ch"),
        P(None, "ch"),
        P("ch"),
        P("ch"),
        P(None, "ch"),
        P(None, "ch"),
        P("ch", None),
    )
    return jax.shard_map(
        local,
        mesh=mesh,
        in_specs=placed,
        out_specs=(P(None, "seq", "ch"), P(None, "seq", "ch")),
        check_vma=False,
    )
```

```python
import jax
import jax.numpy as jnp
from jax import lax
from jax.sharding import PartitionSpec as P


def mirror(value, axes, count):
    return lax.ppermute(value, axes, [(k, count - 1 - k) for k in range(count)])


def partner(value, axis, bit):
    mask = 1 << bit
    return lax.ppermute(value, axis, [(k, k ^ mask) for k in range(lax.axis_size(axis))])


def padded_2(cells, axis, dim, width):
    count = lax.axis_size(axis)
    ends = count - 1
    head = lax.slice_in_dim(cells, 0, width, axis=dim)
    tail = lax.slice_in_dim(cells, cells.shape[dim] - width, cells.shape[dim], axis=dim)
    return jnp.concatenate(
        [
            lax.ppermute(tail, axis, [(i, (i + 1) % count) for i in range(ends)]),
            cells,
            lax.ppermute(head, axis, [((i + 1) % count, i) for i in range(ends)]),
        ],
        axis=dim,
    )


def embedded(bases, table):
    out = jnp.zeros(bases.shape + (table.shape[1],), jnp.float32)
    for v in range(table.shape[0]):
        out = out + jnp.where(bases[..., None] == v, table[v], 0.0)
    return out


def gather_blocks(block, bits, me):
    cur = block[None]
    for bit in reversed(range(bits)):
        other = partner(cur, "ch", bit)
        low = ((me >> bit) & 1) == 0
        first = jnp.where(low, cur, other)
        second = jnp.where(low, other, cur)
        cur = jnp.stack([first, second], axis=1).reshape((-1,) + block.shape)
    return cur


def scatter_blocks(part, bits, me):
    cur = part
    rows, _, w = part.shape
    for bit in range(bits):
        cur = cur.reshape(rows, -1, 2, w)
        low = ((me >> bit) & 1) == 0
        keep = jnp.where(low, cur[:, :, 0], cur[:, :, 1])
        give = jnp.where(low, cur[:, :, 1], cur[:, :, 0])
        if bit > 0:
            give = give.astype(jnp.bfloat16)
        cur = keep + partner(give, "ch", bit).astype(jnp.float32)
    return cur[:, 0]


def reversal(n, block):
    rows = lax.broadcasted_iota(jnp.int32, (n, n), 0)
    cols = lax.broadcasted_iota(jnp.int32, (n, n), 1)
    same = rows // block == cols // block
    return (same & (rows % block + cols % block == block - 1)).astype(jnp.bfloat16)


def local(
    tokens,
    masked,
    hidden_forward,
    hidden_reverse,
    embed_table,
    conv_kernel,
    conv_bias,
    norm_gain,
    w_gate,
    w_value,
    w_out,
):
    seq_count = lax.axis_size("seq")
    ch_count = lax.axis_size("ch")
    ch_bits = ch_count.bit_length() - 1
    me = lax.axis_index("ch")
    table = embed_table.astype(jnp.float32)
    base_in = jnp.where(masked == 1, 4, tokens)
    comp = jnp.where(masked == 1, 4, 3 - tokens)
    comp_back = jnp.flip(mirror(comp, "seq", seq_count), axis=1)

    local_width = hidden_forward.shape[-1]
    width = local_width * ch_count
    taps = conv_kernel.shape[0]
    half_width = taps // 2

    x_fwd = hidden_forward.astype(jnp.float32) + embedded(base_in, table)
    x_rev = lax.optimization_barrier(hidden_reverse.astype(jnp.float32) + embedded(comp_back, table))
    square_fwd, square_rev = lax.psum(
        (jnp.sum(x_fwd * x_fwd, axis=-1), jnp.sum(x_rev * x_rev, axis=-1)), "ch"
    )
    normed_fwd = (x_fwd * lax.rsqrt(square_fwd[..., None] / width + 1e-05) * norm_gain).astype(
        jnp.bfloat16
    )
    normed_rev = (x_rev * lax.rsqrt(square_rev[..., None] / width + 1e-05) * norm_gain).astype(
        jnp.bfloat16
    )
    stacked = jnp.stack([normed_fwd, normed_rev])
    length = stacked.shape[2]
    padded = padded_2(stacked, "seq", 2, half_width).astype(jnp.float32)
    conv = jnp.zeros(stacked.shape, jnp.float32) + conv_bias
    for offset in range(taps):
        conv = conv + conv_kernel[offset] * padded[:, :, offset : offset + length]
    conv = conv.astype(jnp.bfloat16)
    rows_fwd = conv[0].reshape(-1, local_width)
    rows_all = rows_fwd.shape[0]
    turned_rev = jnp.dot(
        reversal(rows_all, length), conv[1].reshape(rows_all, -1), preferred_element_type=jnp.float32
    ).astype(jnp.bfloat16)
    rows_fwd, turned_rev = lax.optimization_barrier((rows_fwd, turned_rev))
    rows_rev = mirror(turned_rev, "seq", seq_count)

    def activation(rows):
        pieces = gather_blocks(rows, ch_bits, me)
        dims = (((0, 2), (0, 1)), ((), ()))
        gate = lax.dot_general(
            pieces, w_gate.reshape(ch_count, local_width, -1), dims, preferred_element_type=jnp.float32
        )
        value = lax.dot_general(
            pieces, w_value.reshape(ch_count, local_width, -1), dims, preferred_element_type=jnp.float32
        )
        return (jax.nn.silu(gate) * value).astype(jnp.bfloat16)

    act_fwd = activation(rows_fwd)
    part_fwd = jnp.dot(act_fwd, w_out, preferred_element_type=jnp.float32)
    w_flip = jnp.dot(w_out, reversal(width, width), preferred_element_type=jnp.float32).astype(jnp.bfloat16)
    rows_rev, part_fwd, w_flip = lax.optimization_barrier((rows_rev, part_fwd, w_flip))
    act_rev = activation(rows_rev)
    lane_flip = reversal(local_width, local_width)
    part = part_fwd + jnp.dot(act_rev, w_flip, preferred_element_type=jnp.float32)
    share = scatter_blocks(part.reshape(part.shape[0], ch_count, local_width), ch_bits, me)
    out_forward = x_fwd + share.reshape(x_fwd.shape)
    row_flip = reversal(share.shape[0], x_fwd.shape[1])
    turned = jnp.dot(share.astype(jnp.bfloat16), lane_flip, preferred_element_type=jnp.float32)
    turned = jnp.dot(row_flip, turned.astype(jnp.bfloat16), preferred_element_type=jnp.float32)
    sent = mirror(turned.astype(jnp.bfloat16).reshape(x_fwd.shape), ("seq", "ch"), seq_count * ch_count)
    out_reverse = x_rev + sent.astype(jnp.float32)
    return (out_forward.astype(jnp.bfloat16), out_reverse.astype(jnp.bfloat16))


def solution(mesh):
    placed = (
        P(None, "seq"),
        P(None, "seq"),
        P(None, "seq", "ch"),
        P(None, "seq", "ch"),
        P(None, "ch"),
        P(None, "ch"),
        P("ch"),
        P("ch"),
        P(None, "ch"),
        P(None, "ch"),
        P("ch", None),
    )
    return jax.shard_map(
        local,
        mesh=mesh,
        in_specs=placed,
        out_specs=(P(None, "seq", "ch"), P(None, "seq", "ch")),
        check_vma=False,
    )
```

```python
import jax
import jax.numpy as jnp
from jax import lax
from jax.sharding import PartitionSpec as P


def mirror(value, axes, count):
    return lax.ppermute(value, axes, [(k, count - 1 - k) for k in range(count)])


def partner(value, axis, bit):
    mask = 1 << bit
    return lax.ppermute(value, axis, [(k, k ^ mask) for k in range(lax.axis_size(axis))])


def padded_2(cells, axis, dim, width):
    count = lax.axis_size(axis)
    ends = count - 1
    head = lax.slice_in_dim(cells, 0, width, axis=dim)
    tail = lax.slice_in_dim(cells, cells.shape[dim] - width, cells.shape[dim], axis=dim)
    return jnp.concatenate(
        [
            lax.ppermute(tail, axis, [(i, (i + 1) % count) for i in range(ends)]),
            cells,
            lax.ppermute(head, axis, [((i + 1) % count, i) for i in range(ends)]),
        ],
        axis=dim,
    )


def embedded(bases, table):
    out = jnp.zeros(bases.shape + (table.shape[1],), jnp.float32)
    for v in range(table.shape[0]):
        out = out + jnp.where(bases[..., None] == v, table[v], 0.0)
    return out


def gather_blocks(block, bits, me):
    cur = block[None]
    for bit in reversed(range(bits)):
        other = partner(cur, "ch", bit)
        low = ((me >> bit) & 1) == 0
        first = jnp.where(low, cur, other)
        second = jnp.where(low, other, cur)
        cur = jnp.stack([first, second], axis=1).reshape((-1,) + block.shape)
    return cur


def scatter_blocks(part, bits, me):
    cur = part
    rows, _, w = part.shape
    for bit in range(bits):
        cur = cur.reshape(rows, -1, 2, w)
        low = ((me >> bit) & 1) == 0
        keep = jnp.where(low, cur[:, :, 0], cur[:, :, 1])
        give = jnp.where(low, cur[:, :, 1], cur[:, :, 0])
        if bit > 0:
            give = give.astype(jnp.bfloat16)
        cur = keep + partner(give, "ch", bit).astype(jnp.float32)
    return cur[:, 0]


def reversal(n, block):
    rows = lax.broadcasted_iota(jnp.int32, (n, n), 0)
    cols = lax.broadcasted_iota(jnp.int32, (n, n), 1)
    same = rows // block == cols // block
    return (same & (rows % block + cols % block == block - 1)).astype(jnp.bfloat16)


def local(
    tokens,
    masked,
    hidden_forward,
    hidden_reverse,
    embed_table,
    conv_kernel,
    conv_bias,
    norm_gain,
    w_gate,
    w_value,
    w_out,
):
    seq_count = lax.axis_size("seq")
    ch_count = lax.axis_size("ch")
    ch_bits = ch_count.bit_length() - 1
    me = lax.axis_index("ch")
    table = embed_table.astype(jnp.float32)
    base_in = jnp.where(masked == 1, 4, tokens)
    comp = jnp.where(masked == 1, 4, 3 - tokens)
    comp_back = jnp.flip(mirror(comp, "seq", seq_count), axis=1)

    local_width = hidden_forward.shape[-1]
    width = local_width * ch_count
    taps = conv_kernel.shape[0]
    half_width = taps // 2

    x_fwd = hidden_forward.astype(jnp.float32) + embedded(base_in, table)
    x_rev = lax.optimization_barrier(hidden_reverse.astype(jnp.float32) + embedded(comp_back, table))
    square_fwd, square_rev = lax.psum(
        (jnp.sum(x_fwd * x_fwd, axis=-1), jnp.sum(x_rev * x_rev, axis=-1)), "ch"
    )
    normed_fwd = (x_fwd * lax.rsqrt(square_fwd[..., None] / width + 1e-05) * norm_gain).astype(
        jnp.bfloat16
    )
    normed_rev = (x_rev * lax.rsqrt(square_rev[..., None] / width + 1e-05) * norm_gain).astype(
        jnp.bfloat16
    )
    stacked = jnp.stack([normed_fwd, normed_rev])
    length = stacked.shape[2]
    padded = padded_2(stacked, "seq", 2, half_width).astype(jnp.float32)
    conv = jnp.zeros(stacked.shape, jnp.float32) + conv_bias
    for offset in range(taps):
        conv = conv + conv_kernel[offset] * padded[:, :, offset : offset + length]
    conv = conv.astype(jnp.bfloat16)
    rows_fwd = conv[0].reshape(-1, local_width)
    rows_all = rows_fwd.shape[0]
    rows_rev = mirror(
        jnp.dot(
            reversal(rows_all, length), conv[1].reshape(rows_all, -1), preferred_element_type=jnp.float32
        ).astype(jnp.bfloat16),
        "seq",
        seq_count,
    )

    def activation(rows):
        pieces = gather_blocks(rows, ch_bits, me)
        dims = (((0, 2), (0, 1)), ((), ()))
        gate = lax.dot_general(
            pieces, w_gate.reshape(ch_count, local_width, -1), dims, preferred_element_type=jnp.float32
        )
        value = lax.dot_general(
            pieces, w_value.reshape(ch_count, local_width, -1), dims, preferred_element_type=jnp.float32
        )
        return (jax.nn.silu(gate) * value).astype(jnp.bfloat16)

    act_fwd = activation(rows_fwd)
    act_rev = activation(rows_rev)
    lane_flip = reversal(local_width, local_width)
    w_flip = jnp.dot(w_out, reversal(width, width), preferred_element_type=jnp.float32).astype(jnp.bfloat16)
    part = jnp.dot(act_fwd, w_out, preferred_element_type=jnp.float32) + jnp.dot(
        act_rev, w_flip, preferred_element_type=jnp.float32
    )
    share = scatter_blocks(part.reshape(part.shape[0], ch_count, local_width), ch_bits, me)
    out_forward = x_fwd + share.reshape(x_fwd.shape)
    row_flip = reversal(share.shape[0], x_fwd.shape[1])
    turned = jnp.dot(share.astype(jnp.bfloat16), lane_flip, preferred_element_type=jnp.float32)
    turned = jnp.dot(row_flip, turned.astype(jnp.bfloat16), preferred_element_type=jnp.float32)
    sent = mirror(turned.astype(jnp.bfloat16).reshape(x_fwd.shape), ("seq", "ch"), seq_count * ch_count)
    out_reverse = x_rev + sent.astype(jnp.float32)
    return (out_forward.astype(jnp.bfloat16), out_reverse.astype(jnp.bfloat16))


def solution(mesh):
    placed = (
        P(None, "seq"),
        P(None, "seq"),
        P(None, "seq", "ch"),
        P(None, "seq", "ch"),
        P(None, "ch"),
        P(None, "ch"),
        P("ch"),
        P("ch"),
        P(None, "ch"),
        P(None, "ch"),
        P("ch", None),
    )
    return jax.shard_map(
        local,
        mesh=mesh,
        in_specs=placed,
        out_specs=(P(None, "seq", "ch"), P(None, "seq", "ch")),
        check_vma=False,
    )
```

```python
import jax
import jax.numpy as jnp
from jax import lax
from jax.sharding import PartitionSpec as P


def mirror(value, axes, count):
    return lax.ppermute(value, axes, [(k, count - 1 - k) for k in range(count)])


def partner(value, axis, bit):
    mask = 1 << bit
    return lax.ppermute(value, axis, [(k, k ^ mask) for k in range(lax.axis_size(axis))])


def padded_2(cells, axis, dim, width):
    count = lax.axis_size(axis)
    ends = count - 1
    head = lax.slice_in_dim(cells, 0, width, axis=dim)
    tail = lax.slice_in_dim(cells, cells.shape[dim] - width, cells.shape[dim], axis=dim)
    return jnp.concatenate(
        [
            lax.ppermute(tail, axis, [(i, (i + 1) % count) for i in range(ends)]),
            cells,
            lax.ppermute(head, axis, [((i + 1) % count, i) for i in range(ends)]),
        ],
        axis=dim,
    )


def embedded(bases, table):
    out = jnp.zeros(bases.shape + (table.shape[1],), jnp.float32)
    for v in range(table.shape[0]):
        out = out + jnp.where(bases[..., None] == v, table[v], 0.0)
    return out


def gather_blocks(block, bits, me):
    cur = block[None]
    for bit in reversed(range(bits)):
        other = partner(cur, "ch", bit)
        high = (me >> bit) & 1
        both = jnp.stack([cur, other, cur], axis=1)
        cur = lax.dynamic_slice_in_dim(both, high, 2, axis=1).reshape((-1,) + block.shape)
    return cur


def scatter_blocks(part, bits, me):
    cur = part
    rows, _, w = part.shape
    for bit in range(bits):
        cur = cur.reshape(rows, -1, 2, w)
        high = (me >> bit) & 1
        keep = lax.dynamic_index_in_dim(cur, high, axis=2, keepdims=False)
        give = lax.dynamic_index_in_dim(cur, 1 - high, axis=2, keepdims=False)
        if bit > 0:
            give = give.astype(jnp.bfloat16)
        cur = keep + partner(give, "ch", bit).astype(jnp.float32)
    return cur[:, 0]


def reversal(n, block):
    rows = lax.broadcasted_iota(jnp.int32, (n, n), 0)
    cols = lax.broadcasted_iota(jnp.int32, (n, n), 1)
    same = rows // block == cols // block
    return (same & (rows % block + cols % block == block - 1)).astype(jnp.bfloat16)


def local(
    tokens,
    masked,
    hidden_forward,
    hidden_reverse,
    embed_table,
    conv_kernel,
    conv_bias,
    norm_gain,
    w_gate,
    w_value,
    w_out,
):
    seq_count = lax.axis_size("seq")
    ch_count = lax.axis_size("ch")
    ch_bits = ch_count.bit_length() - 1
    me = lax.axis_index("ch")
    table = embed_table.astype(jnp.float32)
    base_in = jnp.where(masked == 1, 4, tokens)
    comp = jnp.where(masked == 1, 4, 3 - tokens)
    comp_back = jnp.flip(mirror(comp, "seq", seq_count), axis=1)

    local_width = hidden_forward.shape[-1]
    width = local_width * ch_count
    taps = conv_kernel.shape[0]
    half_width = taps // 2

    x_fwd = hidden_forward.astype(jnp.float32) + embedded(base_in, table)
    x_rev = lax.optimization_barrier(hidden_reverse.astype(jnp.float32) + embedded(comp_back, table))
    square_fwd, square_rev = lax.psum(
        (jnp.sum(x_fwd * x_fwd, axis=-1), jnp.sum(x_rev * x_rev, axis=-1)), "ch"
    )
    normed_fwd = (x_fwd * lax.rsqrt(square_fwd[..., None] / width + 1e-05) * norm_gain).astype(
        jnp.bfloat16
    )
    normed_rev = (x_rev * lax.rsqrt(square_rev[..., None] / width + 1e-05) * norm_gain).astype(
        jnp.bfloat16
    )
    stacked = jnp.stack([normed_fwd, normed_rev])
    length = stacked.shape[2]
    padded = padded_2(stacked, "seq", 2, half_width).astype(jnp.float32)
    conv = jnp.zeros(stacked.shape, jnp.float32) + conv_bias
    for offset in range(taps):
        conv = conv + conv_kernel[offset] * padded[:, :, offset : offset + length]
    conv = conv.astype(jnp.bfloat16)
    rows_fwd = conv[0].reshape(-1, local_width)
    rows_all = rows_fwd.shape[0]
    rows_rev = mirror(
        jnp.dot(
            reversal(rows_all, length), conv[1].reshape(rows_all, -1), preferred_element_type=jnp.float32
        ).astype(jnp.bfloat16),
        "seq",
        seq_count,
    )

    def activation(rows):
        pieces = gather_blocks(rows, ch_bits, me)
        dims = (((0, 2), (0, 1)), ((), ()))
        gate = lax.dot_general(
            pieces, w_gate.reshape(ch_count, local_width, -1), dims, preferred_element_type=jnp.float32
        )
        value = lax.dot_general(
            pieces, w_value.reshape(ch_count, local_width, -1), dims, preferred_element_type=jnp.float32
        )
        return (jax.nn.silu(gate) * value).astype(jnp.bfloat16)

    act_fwd = activation(rows_fwd)
    act_rev = activation(rows_rev)
    lane_flip = reversal(local_width, local_width)
    w_flip = jnp.dot(w_out, reversal(width, width), preferred_element_type=jnp.float32).astype(jnp.bfloat16)
    part = jnp.dot(act_fwd, w_out, preferred_element_type=jnp.float32) + jnp.dot(
        act_rev, w_flip, preferred_element_type=jnp.float32
    )
    share = scatter_blocks(part.reshape(part.shape[0], ch_count, local_width), ch_bits, me)
    out_forward = x_fwd + share.reshape(x_fwd.shape)
    row_flip = reversal(share.shape[0], x_fwd.shape[1])
    turned = jnp.dot(share.astype(jnp.bfloat16), lane_flip, preferred_element_type=jnp.float32)
    turned = jnp.dot(row_flip, turned.astype(jnp.bfloat16), preferred_element_type=jnp.float32)
    sent = mirror(turned.astype(jnp.bfloat16).reshape(x_fwd.shape), ("seq", "ch"), seq_count * ch_count)
    out_reverse = x_rev + sent.astype(jnp.float32)
    return (out_forward.astype(jnp.bfloat16), out_reverse.astype(jnp.bfloat16))


def solution(mesh):
    placed = (
        P(None, "seq"),
        P(None, "seq"),
        P(None, "seq", "ch"),
        P(None, "seq", "ch"),
        P(None, "ch"),
        P(None, "ch"),
        P("ch"),
        P("ch"),
        P(None, "ch"),
        P(None, "ch"),
        P("ch", None),
    )
    return jax.shard_map(
        local,
        mesh=mesh,
        in_specs=placed,
        out_specs=(P(None, "seq", "ch"), P(None, "seq", "ch")),
        check_vma=False,
    )
```

```python
import jax
import jax.numpy as jnp
from jax import lax
from jax.sharding import PartitionSpec as P


def mirror(value, axes, count):
    return lax.ppermute(value, axes, [(k, count - 1 - k) for k in range(count)])


def partner(value, axis, bit):
    mask = 1 << bit
    return lax.ppermute(value, axis, [(k, k ^ mask) for k in range(lax.axis_size(axis))])


def padded_2(cells, axis, dim, width):
    count = lax.axis_size(axis)
    ends = count - 1
    head = lax.slice_in_dim(cells, 0, width, axis=dim)
    tail = lax.slice_in_dim(cells, cells.shape[dim] - width, cells.shape[dim], axis=dim)
    return jnp.concatenate(
        [
            lax.ppermute(tail, axis, [(i, (i + 1) % count) for i in range(ends)]),
            cells,
            lax.ppermute(head, axis, [((i + 1) % count, i) for i in range(ends)]),
        ],
        axis=dim,
    )


def embedded(bases, table):
    out = jnp.zeros(bases.shape + (table.shape[1],), jnp.float32)
    for v in range(table.shape[0]):
        out = out + jnp.where(bases[..., None] == v, table[v], 0.0)
    return out


def gather_blocks(block, bits, me):
    cur = block[None]
    for bit in reversed(range(bits)):
        other = partner(cur, "ch", bit)
        low = ((me >> bit) & 1) == 0
        first = jnp.where(low, cur, other)
        second = jnp.where(low, other, cur)
        cur = jnp.stack([first, second], axis=1).reshape((-1,) + block.shape)
    return cur


def scatter_blocks(part, bits, me):
    cur = part
    rows, _, w = part.shape
    for bit in range(bits):
        cur = cur.reshape(rows, -1, 2, w)
        low = ((me >> bit) & 1) == 0
        keep = jnp.where(low, cur[:, :, 0], cur[:, :, 1])
        give = jnp.where(low, cur[:, :, 1], cur[:, :, 0])
        if bit > 0:
            give = give.astype(jnp.bfloat16)
        cur = keep + partner(give, "ch", bit).astype(jnp.float32)
    return cur[:, 0]


def reversal(n, block):
    rows = lax.broadcasted_iota(jnp.int32, (n, n), 0)
    cols = lax.broadcasted_iota(jnp.int32, (n, n), 1)
    same = rows // block == cols // block
    return (same & (rows % block + cols % block == block - 1)).astype(jnp.bfloat16)


def local(
    tokens,
    masked,
    hidden_forward,
    hidden_reverse,
    embed_table,
    conv_kernel,
    conv_bias,
    norm_gain,
    w_gate,
    w_value,
    w_out,
):
    seq_count = lax.axis_size("seq")
    ch_count = lax.axis_size("ch")
    ch_bits = ch_count.bit_length() - 1
    me = lax.axis_index("ch")
    table = embed_table.astype(jnp.float32)
    base_in = jnp.where(masked == 1, 4, tokens)
    comp = jnp.where(masked == 1, 4, 3 - tokens)
    comp_back = jnp.flip(mirror(comp, "seq", seq_count), axis=1)

    local_width = hidden_forward.shape[-1]
    width = local_width * ch_count
    taps = conv_kernel.shape[0]
    half_width = taps // 2

    x_fwd = hidden_forward.astype(jnp.float32) + embedded(base_in, table)
    x_rev = lax.optimization_barrier(hidden_reverse.astype(jnp.float32) + embedded(comp_back, table))
    square_fwd, square_rev = lax.psum(
        (jnp.sum(x_fwd * x_fwd, axis=-1), jnp.sum(x_rev * x_rev, axis=-1)), "ch"
    )
    normed_fwd = (x_fwd * lax.rsqrt(square_fwd[..., None] / width + 1e-05) * norm_gain).astype(
        jnp.bfloat16
    )
    normed_rev = (x_rev * lax.rsqrt(square_rev[..., None] / width + 1e-05) * norm_gain).astype(
        jnp.bfloat16
    )
    stacked = jnp.stack([normed_fwd, normed_rev])
    length = stacked.shape[2]
    padded = padded_2(stacked, "seq", 2, half_width).astype(jnp.float32)
    conv = jnp.zeros(stacked.shape, jnp.float32) + conv_bias
    for offset in range(taps):
        conv = conv + conv_kernel[offset] * padded[:, :, offset : offset + length]
    conv = conv.astype(jnp.bfloat16)
    rows_fwd = conv[0].reshape(-1, local_width)
    rows_all = rows_fwd.shape[0]
    rows_rev = mirror(
        jnp.dot(
            reversal(rows_all, length), conv[1].reshape(rows_all, -1), preferred_element_type=jnp.float32
        ).astype(jnp.bfloat16),
        "seq",
        seq_count,
    )

    def activation(rows):
        pieces = gather_blocks(rows, ch_bits, me)
        dims = (((0, 2), (0, 1)), ((), ()))
        gate = lax.dot_general(
            pieces, w_gate.reshape(ch_count, local_width, -1), dims, preferred_element_type=jnp.float32
        )
        value = lax.dot_general(
            pieces, w_value.reshape(ch_count, local_width, -1), dims, preferred_element_type=jnp.float32
        )
        return (jax.nn.silu(gate) * value).astype(jnp.bfloat16)

    w_flip = jnp.dot(w_out, reversal(width, width), preferred_element_type=jnp.float32).astype(jnp.bfloat16)
    rows_rev, w_flip = lax.optimization_barrier((rows_rev, w_flip))
    act_fwd = activation(rows_fwd)
    act_rev = activation(rows_rev)
    lane_flip = reversal(local_width, local_width)
    part = jnp.dot(act_fwd, w_out, preferred_element_type=jnp.float32) + jnp.dot(
        act_rev, w_flip, preferred_element_type=jnp.float32
    )
    share = scatter_blocks(part.reshape(part.shape[0], ch_count, local_width), ch_bits, me)
    out_forward = x_fwd + share.reshape(x_fwd.shape)
    row_flip = reversal(share.shape[0], x_fwd.shape[1])
    turned = jnp.dot(share.astype(jnp.bfloat16), lane_flip, preferred_element_type=jnp.float32)
    turned = jnp.dot(row_flip, turned.astype(jnp.bfloat16), preferred_element_type=jnp.float32)
    sent = mirror(turned.astype(jnp.bfloat16).reshape(x_fwd.shape), ("seq", "ch"), seq_count * ch_count)
    out_reverse = x_rev + sent.astype(jnp.float32)
    return (out_forward.astype(jnp.bfloat16), out_reverse.astype(jnp.bfloat16))


def solution(mesh):
    placed = (
        P(None, "seq"),
        P(None, "seq"),
        P(None, "seq", "ch"),
        P(None, "seq", "ch"),
        P(None, "ch"),
        P(None, "ch"),
        P("ch"),
        P("ch"),
        P(None, "ch"),
        P(None, "ch"),
        P("ch", None),
    )
    return jax.shard_map(
        local,
        mesh=mesh,
        in_specs=placed,
        out_specs=(P(None, "seq", "ch"), P(None, "seq", "ch")),
        check_vma=False,
    )
```

```python
import jax
import jax.numpy as jnp
from jax import lax
from jax.sharding import PartitionSpec as P


def mirror(value, axes, count):
    return lax.ppermute(value, axes, [(k, count - 1 - k) for k in range(count)])


def partner(value, axis, bit):
    mask = 1 << bit
    return lax.ppermute(value, axis, [(k, k ^ mask) for k in range(lax.axis_size(axis))])


def padded_2(cells, axis, dim, width):
    count = lax.axis_size(axis)
    ends = count - 1
    head = lax.slice_in_dim(cells, 0, width, axis=dim)
    tail = lax.slice_in_dim(cells, cells.shape[dim] - width, cells.shape[dim], axis=dim)
    return jnp.concatenate(
        [
            lax.ppermute(tail, axis, [(i, (i + 1) % count) for i in range(ends)]),
            cells,
            lax.ppermute(head, axis, [((i + 1) % count, i) for i in range(ends)]),
        ],
        axis=dim,
    )


def embedded(bases, table):
    out = jnp.zeros(bases.shape + (table.shape[1],), jnp.float32)
    for v in range(table.shape[0]):
        out = out + jnp.where(bases[..., None] == v, table[v], 0.0)
    return out


def gather_blocks(block, bits, me):
    cur = block[None]
    for bit in reversed(range(bits)):
        other = partner(cur, "ch", bit)
        low = ((me >> bit) & 1) == 0
        first = jnp.where(low, cur, other)
        second = jnp.where(low, other, cur)
        cur = jnp.stack([first, second], axis=1).reshape((-1,) + block.shape)
    return cur


def scatter_blocks(part, bits, me):
    cur = part
    rows, _, w = part.shape
    for bit in range(bits):
        cur = cur.reshape(rows, -1, 2, w)
        low = ((me >> bit) & 1) == 0
        keep = jnp.where(low, cur[:, :, 0], cur[:, :, 1])
        give = jnp.where(low, cur[:, :, 1], cur[:, :, 0])
        cur = keep + partner(give.astype(jnp.bfloat16), "ch", bit).astype(jnp.float32)
    return cur[:, 0]


def reversal(n, block):
    rows = lax.broadcasted_iota(jnp.int32, (n, n), 0)
    cols = lax.broadcasted_iota(jnp.int32, (n, n), 1)
    same = rows // block == cols // block
    return (same & (rows % block + cols % block == block - 1)).astype(jnp.bfloat16)


def local(
    tokens,
    masked,
    hidden_forward,
    hidden_reverse,
    embed_table,
    conv_kernel,
    conv_bias,
    norm_gain,
    w_gate,
    w_value,
    w_out,
):
    seq_count = lax.axis_size("seq")
    ch_count = lax.axis_size("ch")
    ch_bits = ch_count.bit_length() - 1
    me = lax.axis_index("ch")
    table = embed_table.astype(jnp.float32)
    base_in = jnp.where(masked == 1, 4, tokens)
    comp = jnp.where(masked == 1, 4, 3 - tokens)
    comp_back = jnp.flip(mirror(comp, "seq", seq_count), axis=1)

    local_width = hidden_forward.shape[-1]
    width = local_width * ch_count
    taps = conv_kernel.shape[0]
    half_width = taps // 2

    x_fwd = hidden_forward.astype(jnp.float32) + embedded(base_in, table)
    x_rev = lax.optimization_barrier(hidden_reverse.astype(jnp.float32) + embedded(comp_back, table))
    square_fwd, square_rev = lax.psum(
        (jnp.sum(x_fwd * x_fwd, axis=-1), jnp.sum(x_rev * x_rev, axis=-1)), "ch"
    )
    normed_fwd = (x_fwd * lax.rsqrt(square_fwd[..., None] / width + 1e-05) * norm_gain).astype(
        jnp.bfloat16
    )
    normed_rev = (x_rev * lax.rsqrt(square_rev[..., None] / width + 1e-05) * norm_gain).astype(
        jnp.bfloat16
    )
    stacked = jnp.stack([normed_fwd, normed_rev])
    length = stacked.shape[2]
    padded = padded_2(stacked, "seq", 2, half_width).astype(jnp.float32)
    conv = jnp.zeros(stacked.shape, jnp.float32) + conv_bias
    for offset in range(taps):
        conv = conv + conv_kernel[offset] * padded[:, :, offset : offset + length]
    conv = conv.astype(jnp.bfloat16)
    rows_fwd = conv[0].reshape(-1, local_width)
    rows_all = rows_fwd.shape[0]
    rows_rev = mirror(
        jnp.dot(
            reversal(rows_all, length), conv[1].reshape(rows_all, -1), preferred_element_type=jnp.float32
        ).astype(jnp.bfloat16),
        "seq",
        seq_count,
    )

    def activation(rows):
        pieces = gather_blocks(rows, ch_bits, me)
        dims = (((0, 2), (0, 1)), ((), ()))
        gate = lax.dot_general(
            pieces, w_gate.reshape(ch_count, local_width, -1), dims, preferred_element_type=jnp.float32
        )
        value = lax.dot_general(
            pieces, w_value.reshape(ch_count, local_width, -1), dims, preferred_element_type=jnp.float32
        )
        return (jax.nn.silu(gate) * value).astype(jnp.bfloat16)

    act_fwd = activation(rows_fwd)
    act_rev = activation(rows_rev)
    lane_flip = reversal(local_width, local_width)
    w_flip = jnp.dot(w_out, reversal(width, width), preferred_element_type=jnp.float32).astype(jnp.bfloat16)
    part = jnp.dot(act_fwd, w_out, preferred_element_type=jnp.float32) + jnp.dot(
        act_rev, w_flip, preferred_element_type=jnp.float32
    )
    share = scatter_blocks(part.reshape(part.shape[0], ch_count, local_width), ch_bits, me)
    out_forward = x_fwd + share.reshape(x_fwd.shape)
    row_flip = reversal(share.shape[0], x_fwd.shape[1])
    turned = jnp.dot(share.astype(jnp.bfloat16), lane_flip, preferred_element_type=jnp.float32)
    turned = jnp.dot(row_flip, turned.astype(jnp.bfloat16), preferred_element_type=jnp.float32)
    sent = mirror(turned.astype(jnp.bfloat16).reshape(x_fwd.shape), ("seq", "ch"), seq_count * ch_count)
    out_reverse = x_rev + sent.astype(jnp.float32)
    return (out_forward.astype(jnp.bfloat16), out_reverse.astype(jnp.bfloat16))


def solution(mesh):
    placed = (
        P(None, "seq"),
        P(None, "seq"),
        P(None, "seq", "ch"),
        P(None, "seq", "ch"),
        P(None, "ch"),
        P(None, "ch"),
        P("ch"),
        P("ch"),
        P(None, "ch"),
        P(None, "ch"),
        P("ch", None),
    )
    return jax.shard_map(
        local,
        mesh=mesh,
        in_specs=placed,
        out_specs=(P(None, "seq", "ch"), P(None, "seq", "ch")),
        check_vma=False,
    )
```

```python
import jax
import jax.numpy as jnp
from jax import lax
from jax.sharding import PartitionSpec as P


def mirror(value, axes, count):
    return lax.ppermute(value, axes, [(k, count - 1 - k) for k in range(count)])


def partner(value, axis, bit):
    mask = 1 << bit
    return lax.ppermute(value, axis, [(k, k ^ mask) for k in range(lax.axis_size(axis))])


def padded_2(cells, axis, dim, width):
    count = lax.axis_size(axis)
    ends = count - 1
    head = lax.slice_in_dim(cells, 0, width, axis=dim)
    tail = lax.slice_in_dim(cells, cells.shape[dim] - width, cells.shape[dim], axis=dim)
    return jnp.concatenate(
        [
            lax.ppermute(tail, axis, [(i, (i + 1) % count) for i in range(ends)]),
            cells,
            lax.ppermute(head, axis, [((i + 1) % count, i) for i in range(ends)]),
        ],
        axis=dim,
    )


def embedded(bases, table):
    out = jnp.zeros(bases.shape + (table.shape[1],), jnp.float32)
    for v in range(table.shape[0]):
        out = out + jnp.where(bases[..., None] == v, table[v], 0.0)
    return out


def gather_blocks(block, bits, me):
    cur = block[None]
    for bit in reversed(range(bits)):
        other = partner(cur, "ch", bit)
        low = ((me >> bit) & 1) == 0
        first = jnp.where(low, cur, other)
        second = jnp.where(low, other, cur)
        cur = jnp.stack([first, second], axis=1).reshape((-1,) + block.shape)
    return cur


def scatter_blocks(part, bits, me):
    cur = part
    rows, _, w = part.shape
    for bit in range(bits):
        cur = cur.reshape(rows, -1, 2, w)
        low = ((me >> bit) & 1) == 0
        keep = jnp.where(low, cur[:, :, 0], cur[:, :, 1])
        give = jnp.where(low, cur[:, :, 1], cur[:, :, 0])
        if bit > 0:
            give = give.astype(jnp.bfloat16)
        cur = keep + partner(give, "ch", bit).astype(jnp.float32)
    return cur[:, 0]


def flip_rows(values):
    batch, rows, _ = values.shape
    turn = jnp.broadcast_to(reversal(rows, rows), (batch, rows, rows))
    return lax.dot_general(
        turn, values, (((2,), (1,)), ((0,), (0,))), preferred_element_type=jnp.float32
    ).astype(jnp.bfloat16)


def reversal(n, block):
    rows = lax.broadcasted_iota(jnp.int32, (n, n), 0)
    cols = lax.broadcasted_iota(jnp.int32, (n, n), 1)
    same = rows // block == cols // block
    return (same & (rows % block + cols % block == block - 1)).astype(jnp.bfloat16)


def local(
    tokens,
    masked,
    hidden_forward,
    hidden_reverse,
    embed_table,
    conv_kernel,
    conv_bias,
    norm_gain,
    w_gate,
    w_value,
    w_out,
):
    seq_count = lax.axis_size("seq")
    ch_count = lax.axis_size("ch")
    ch_bits = ch_count.bit_length() - 1
    me = lax.axis_index("ch")
    table = embed_table.astype(jnp.float32)
    base_in = jnp.where(masked == 1, 4, tokens)
    comp = jnp.where(masked == 1, 4, 3 - tokens)
    comp_back = jnp.flip(mirror(comp, "seq", seq_count), axis=1)

    local_width = hidden_forward.shape[-1]
    width = local_width * ch_count
    taps = conv_kernel.shape[0]
    half_width = taps // 2

    x_fwd = hidden_forward.astype(jnp.float32) + embedded(base_in, table)
    x_rev = lax.optimization_barrier(hidden_reverse.astype(jnp.float32) + embedded(comp_back, table))
    square_fwd, square_rev = lax.psum(
        (jnp.sum(x_fwd * x_fwd, axis=-1), jnp.sum(x_rev * x_rev, axis=-1)), "ch"
    )
    normed_fwd = (x_fwd * lax.rsqrt(square_fwd[..., None] / width + 1e-05) * norm_gain).astype(
        jnp.bfloat16
    )
    normed_rev = (x_rev * lax.rsqrt(square_rev[..., None] / width + 1e-05) * norm_gain).astype(
        jnp.bfloat16
    )
    stacked = jnp.stack([normed_fwd, normed_rev])
    length = stacked.shape[2]
    padded = padded_2(stacked, "seq", 2, half_width).astype(jnp.float32)
    conv = jnp.zeros(stacked.shape, jnp.float32) + conv_bias
    for offset in range(taps):
        conv = conv + conv_kernel[offset] * padded[:, :, offset : offset + length]
    conv = conv.astype(jnp.bfloat16)
    rows_fwd = conv[0].reshape(-1, local_width)
    rows_all = rows_fwd.shape[0]
    rows_rev = mirror(
        flip_rows(conv[1]).reshape(rows_all, -1),
        "seq",
        seq_count,
    )

    def activation(rows):
        pieces = gather_blocks(rows, ch_bits, me)
        dims = (((0, 2), (0, 1)), ((), ()))
        gate = lax.dot_general(
            pieces, w_gate.reshape(ch_count, local_width, -1), dims, preferred_element_type=jnp.float32
        )
        value = lax.dot_general(
            pieces, w_value.reshape(ch_count, local_width, -1), dims, preferred_element_type=jnp.float32
        )
        return (jax.nn.silu(gate) * value).astype(jnp.bfloat16)

    act_fwd = activation(rows_fwd)
    act_rev = activation(rows_rev)
    lane_flip = reversal(local_width, local_width)
    w_flip = jnp.dot(w_out, reversal(width, width), preferred_element_type=jnp.float32).astype(jnp.bfloat16)
    part = jnp.dot(act_fwd, w_out, preferred_element_type=jnp.float32) + jnp.dot(
        act_rev, w_flip, preferred_element_type=jnp.float32
    )
    share = scatter_blocks(part.reshape(part.shape[0], ch_count, local_width), ch_bits, me)
    out_forward = x_fwd + share.reshape(x_fwd.shape)
    turned = jnp.dot(share.astype(jnp.bfloat16), lane_flip, preferred_element_type=jnp.float32)
    turned = flip_rows(turned.astype(jnp.bfloat16).reshape(x_fwd.shape))
    sent = mirror(turned, ("seq", "ch"), seq_count * ch_count)
    out_reverse = x_rev + sent.astype(jnp.float32)
    return (out_forward.astype(jnp.bfloat16), out_reverse.astype(jnp.bfloat16))


def solution(mesh):
    placed = (
        P(None, "seq"),
        P(None, "seq"),
        P(None, "seq", "ch"),
        P(None, "seq", "ch"),
        P(None, "ch"),
        P(None, "ch"),
        P("ch"),
        P("ch"),
        P(None, "ch"),
        P(None, "ch"),
        P("ch", None),
    )
    return jax.shard_map(
        local,
        mesh=mesh,
        in_specs=placed,
        out_specs=(P(None, "seq", "ch"), P(None, "seq", "ch")),
        check_vma=False,
    )
```

```python
import jax
import jax.numpy as jnp
from jax import lax
from jax.sharding import PartitionSpec as P


def mirror(value, axes, count):
    return lax.ppermute(value, axes, [(k, count - 1 - k) for k in range(count)])


def partner(value, axis, bit):
    mask = 1 << bit
    return lax.ppermute(value, axis, [(k, k ^ mask) for k in range(lax.axis_size(axis))])


def padded_2(cells, axis, dim, width):
    count = lax.axis_size(axis)
    ends = count - 1
    head = lax.slice_in_dim(cells, 0, width, axis=dim)
    tail = lax.slice_in_dim(cells, cells.shape[dim] - width, cells.shape[dim], axis=dim)
    return jnp.concatenate(
        [
            lax.ppermute(tail, axis, [(i, (i + 1) % count) for i in range(ends)]),
            cells,
            lax.ppermute(head, axis, [((i + 1) % count, i) for i in range(ends)]),
        ],
        axis=dim,
    )


def embedded(bases, table):
    out = jnp.zeros(bases.shape + (table.shape[1],), jnp.float32)
    for v in range(table.shape[0]):
        out = out + jnp.where(bases[..., None] == v, table[v], 0.0)
    return out


def gather_blocks(block, bits, me):
    cur = block[None]
    for bit in reversed(range(bits)):
        other = partner(cur, "ch", bit)
        low = ((me >> bit) & 1) == 0
        first = jnp.where(low, cur, other)
        second = jnp.where(low, other, cur)
        cur = jnp.stack([first, second], axis=1).reshape((-1,) + block.shape)
    return cur


def scatter_blocks(part, bits, me):
    cur = part
    rows, _, w = part.shape
    for bit in range(bits):
        cur = cur.reshape(rows, -1, 2, w)
        low = ((me >> bit) & 1) == 0
        keep = jnp.where(low, cur[:, :, 0], cur[:, :, 1])
        give = jnp.where(low, cur[:, :, 1], cur[:, :, 0])
        if bit > 0:
            give = give.astype(jnp.bfloat16)
        cur = keep + partner(give, "ch", bit).astype(jnp.float32)
    return cur[:, 0]


def flip_rows(values):
    batch, rows, _ = values.shape
    turn = jnp.broadcast_to(reversal(rows, rows), (batch, rows, rows))
    return lax.dot_general(
        turn, values, (((2,), (1,)), ((0,), (0,))), preferred_element_type=jnp.float32
    ).astype(jnp.bfloat16)


def reversal(n, block):
    rows = lax.broadcasted_iota(jnp.int32, (n, n), 0)
    cols = lax.broadcasted_iota(jnp.int32, (n, n), 1)
    same = rows // block == cols // block
    return (same & (rows % block + cols % block == block - 1)).astype(jnp.bfloat16)


def local(
    tokens,
    masked,
    hidden_forward,
    hidden_reverse,
    embed_table,
    conv_kernel,
    conv_bias,
    norm_gain,
    w_gate,
    w_value,
    w_out,
):
    seq_count = lax.axis_size("seq")
    ch_count = lax.axis_size("ch")
    ch_bits = ch_count.bit_length() - 1
    me = lax.axis_index("ch")
    table = embed_table.astype(jnp.float32)
    base_in = jnp.where(masked == 1, 4, tokens)
    comp = jnp.where(masked == 1, 4, 3 - tokens)
    comp_back = jnp.flip(mirror(comp, "seq", seq_count), axis=1)

    local_width = hidden_forward.shape[-1]
    width = local_width * ch_count
    taps = conv_kernel.shape[0]
    half_width = taps // 2

    x_fwd = hidden_forward.astype(jnp.float32) + embedded(base_in, table)
    x_rev = lax.optimization_barrier(hidden_reverse.astype(jnp.float32) + embedded(comp_back, table))
    square_fwd, square_rev = lax.psum(
        (jnp.sum(x_fwd * x_fwd, axis=-1), jnp.sum(x_rev * x_rev, axis=-1)), "ch"
    )
    normed_fwd = (x_fwd * lax.rsqrt(square_fwd[..., None] / width + 1e-05) * norm_gain).astype(
        jnp.bfloat16
    )
    normed_rev = (x_rev * lax.rsqrt(square_rev[..., None] / width + 1e-05) * norm_gain).astype(
        jnp.bfloat16
    )
    stacked = jnp.stack([normed_fwd, normed_rev])
    length = stacked.shape[2]
    padded = padded_2(stacked, "seq", 2, half_width).astype(jnp.float32)
    conv = jnp.zeros(stacked.shape, jnp.float32) + conv_bias
    for offset in range(taps):
        conv = conv + conv_kernel[offset] * padded[:, :, offset : offset + length]
    conv = conv.astype(jnp.bfloat16)
    rows_fwd = conv[0].reshape(-1, local_width)
    rows_all = rows_fwd.shape[0]
    rows_rev = mirror(
        flip_rows(conv[1]).reshape(rows_all, -1),
        "seq",
        seq_count,
    )

    def activation(rows):
        pieces = gather_blocks(rows, ch_bits, me)
        dims = (((0, 2), (0, 1)), ((), ()))
        gate = lax.dot_general(
            pieces, w_gate.reshape(ch_count, local_width, -1), dims, preferred_element_type=jnp.float32
        )
        value = lax.dot_general(
            pieces, w_value.reshape(ch_count, local_width, -1), dims, preferred_element_type=jnp.float32
        )
        return (jax.nn.silu(gate) * value).astype(jnp.bfloat16)

    act_fwd = activation(rows_fwd)
    act_rev = activation(rows_rev)
    lane_flip = reversal(local_width, local_width)
    w_flip = jnp.concatenate(
        [
            jnp.dot(
                w_out[:, k * local_width : (k + 1) * local_width], lane_flip, preferred_element_type=jnp.float32
            ).astype(jnp.bfloat16)
            for k in reversed(range(ch_count))
        ],
        axis=1,
    )
    part = jnp.dot(act_fwd, w_out, preferred_element_type=jnp.float32) + jnp.dot(
        act_rev, w_flip, preferred_element_type=jnp.float32
    )
    share = scatter_blocks(part.reshape(part.shape[0], ch_count, local_width), ch_bits, me)
    out_forward = x_fwd + share.reshape(x_fwd.shape)
    turned = jnp.dot(share.astype(jnp.bfloat16), lane_flip, preferred_element_type=jnp.float32)
    turned = flip_rows(turned.astype(jnp.bfloat16).reshape(x_fwd.shape))
    sent = mirror(turned, ("seq", "ch"), seq_count * ch_count)
    out_reverse = x_rev + sent.astype(jnp.float32)
    return (out_forward.astype(jnp.bfloat16), out_reverse.astype(jnp.bfloat16))


def solution(mesh):
    placed = (
        P(None, "seq"),
        P(None, "seq"),
        P(None, "seq", "ch"),
        P(None, "seq", "ch"),
        P(None, "ch"),
        P(None, "ch"),
        P("ch"),
        P("ch"),
        P(None, "ch"),
        P(None, "ch"),
        P("ch", None),
    )
    return jax.shard_map(
        local,
        mesh=mesh,
        in_specs=placed,
        out_specs=(P(None, "seq", "ch"), P(None, "seq", "ch")),
        check_vma=False,
    )
```

```python
import jax
import jax.numpy as jnp
from jax import lax
from jax.sharding import PartitionSpec as P


def mirror(value, axes, count):
    return lax.ppermute(value, axes, [(k, count - 1 - k) for k in range(count)])


def partner(value, axis, bit):
    mask = 1 << bit
    return lax.ppermute(value, axis, [(k, k ^ mask) for k in range(lax.axis_size(axis))])


def padded_2(cells, axis, dim, width):
    count = lax.axis_size(axis)
    ends = count - 1
    head = lax.slice_in_dim(cells, 0, width, axis=dim)
    tail = lax.slice_in_dim(cells, cells.shape[dim] - width, cells.shape[dim], axis=dim)
    return jnp.concatenate(
        [
            lax.ppermute(tail, axis, [(i, (i + 1) % count) for i in range(ends)]),
            cells,
            lax.ppermute(head, axis, [((i + 1) % count, i) for i in range(ends)]),
        ],
        axis=dim,
    )


def embedded(bases, table):
    out = jnp.zeros(bases.shape + (table.shape[1],), jnp.float32)
    for v in range(table.shape[0]):
        out = out + jnp.where(bases[..., None] == v, table[v], 0.0)
    return out


def gather_blocks(block, bits, me):
    cur = block[None]
    for bit in reversed(range(bits)):
        other = partner(cur, "ch", bit)
        low = ((me >> bit) & 1) == 0
        first = jnp.where(low, cur, other)
        second = jnp.where(low, other, cur)
        cur = jnp.stack([first, second], axis=1).reshape((-1,) + block.shape)
    return cur


def scatter_blocks(part, bits, me):
    cur = part
    rows, _, w = part.shape
    for bit in range(bits):
        cur = cur.reshape(rows, -1, 2, w)
        low = ((me >> bit) & 1) == 0
        keep = jnp.where(low, cur[:, :, 0], cur[:, :, 1])
        give = jnp.where(low, cur[:, :, 1], cur[:, :, 0])
        if bit > 0:
            give = give.astype(jnp.bfloat16)
        cur = keep + partner(give, "ch", bit).astype(jnp.float32)
    return cur[:, 0]


def flip_rows(values):
    batch, rows, _ = values.shape
    turn = jnp.broadcast_to(reversal(rows, rows), (batch, rows, rows))
    return lax.dot_general(
        turn, values, (((2,), (1,)), ((0,), (0,))), preferred_element_type=jnp.float32
    ).astype(jnp.bfloat16)


def reversal(n, block):
    rows = lax.broadcasted_iota(jnp.int32, (n, n), 0)
    cols = lax.broadcasted_iota(jnp.int32, (n, n), 1)
    same = rows // block == cols // block
    return (same & (rows % block + cols % block == block - 1)).astype(jnp.bfloat16)


def local(
    tokens,
    masked,
    hidden_forward,
    hidden_reverse,
    embed_table,
    conv_kernel,
    conv_bias,
    norm_gain,
    w_gate,
    w_value,
    w_out,
):
    seq_count = lax.axis_size("seq")
    ch_count = lax.axis_size("ch")
    ch_bits = ch_count.bit_length() - 1
    me = lax.axis_index("ch")
    table = embed_table.astype(jnp.float32)
    base_in = jnp.where(masked == 1, 4, tokens)
    comp = jnp.where(masked == 1, 4, 3 - tokens)
    comp_back = jnp.flip(mirror(comp, "seq", seq_count), axis=1)

    local_width = hidden_forward.shape[-1]
    width = local_width * ch_count
    taps = conv_kernel.shape[0]
    half_width = taps // 2

    x_fwd = lax.optimization_barrier(hidden_forward.astype(jnp.float32) + embedded(base_in, table))
    x_rev = lax.optimization_barrier(hidden_reverse.astype(jnp.float32) + embedded(comp_back, table))
    square_fwd, square_rev = lax.psum(
        (jnp.sum(x_fwd * x_fwd, axis=-1), jnp.sum(x_rev * x_rev, axis=-1)), "ch"
    )
    normed_fwd = (x_fwd * lax.rsqrt(square_fwd[..., None] / width + 1e-05) * norm_gain).astype(
        jnp.bfloat16
    )
    normed_rev = (x_rev * lax.rsqrt(square_rev[..., None] / width + 1e-05) * norm_gain).astype(
        jnp.bfloat16
    )
    stacked = jnp.stack([normed_fwd, normed_rev])
    length = stacked.shape[2]
    padded = padded_2(stacked, "seq", 2, half_width).astype(jnp.float32)
    conv = jnp.zeros(stacked.shape, jnp.float32) + conv_bias
    for offset in range(taps):
        conv = conv + conv_kernel[offset] * padded[:, :, offset : offset + length]
    conv = conv.astype(jnp.bfloat16)
    rows_fwd = conv[0].reshape(-1, local_width)
    rows_all = rows_fwd.shape[0]
    rows_rev = mirror(
        flip_rows(conv[1]).reshape(rows_all, -1),
        "seq",
        seq_count,
    )

    def activation(rows):
        pieces = gather_blocks(rows, ch_bits, me)
        dims = (((0, 2), (0, 1)), ((), ()))
        gate = lax.dot_general(
            pieces, w_gate.reshape(ch_count, local_width, -1), dims, preferred_element_type=jnp.float32
        )
        value = lax.dot_general(
            pieces, w_value.reshape(ch_count, local_width, -1), dims, preferred_element_type=jnp.float32
        )
        return (jax.nn.silu(gate) * value).astype(jnp.bfloat16)

    act_fwd = activation(rows_fwd)
    act_rev = activation(rows_rev)
    lane_flip = reversal(local_width, local_width)
    w_flip = jnp.dot(w_out, reversal(width, width), preferred_element_type=jnp.float32).astype(jnp.bfloat16)
    part = jnp.dot(act_fwd, w_out, preferred_element_type=jnp.float32) + jnp.dot(
        act_rev, w_flip, preferred_element_type=jnp.float32
    )
    share = scatter_blocks(part.reshape(part.shape[0], ch_count, local_width), ch_bits, me)
    out_forward = x_fwd + share.reshape(x_fwd.shape)
    turned = jnp.dot(share.astype(jnp.bfloat16), lane_flip, preferred_element_type=jnp.float32)
    turned = flip_rows(turned.astype(jnp.bfloat16).reshape(x_fwd.shape))
    sent = mirror(turned, ("seq", "ch"), seq_count * ch_count)
    out_reverse = x_rev + sent.astype(jnp.float32)
    return (out_forward.astype(jnp.bfloat16), out_reverse.astype(jnp.bfloat16))


def solution(mesh):
    placed = (
        P(None, "seq"),
        P(None, "seq"),
        P(None, "seq", "ch"),
        P(None, "seq", "ch"),
        P(None, "ch"),
        P(None, "ch"),
        P("ch"),
        P("ch"),
        P(None, "ch"),
        P(None, "ch"),
        P("ch", None),
    )
    return jax.shard_map(
        local,
        mesh=mesh,
        in_specs=placed,
        out_specs=(P(None, "seq", "ch"), P(None, "seq", "ch")),
        check_vma=False,
    )
```

```python
import jax
import jax.numpy as jnp
from jax import lax
from jax.sharding import PartitionSpec as P


def mirror(value, axes, count):
    return lax.ppermute(value, axes, [(k, count - 1 - k) for k in range(count)])


def partner(value, axis, bit):
    mask = 1 << bit
    return lax.ppermute(value, axis, [(k, k ^ mask) for k in range(lax.axis_size(axis))])


def padded_2(cells, axis, dim, width):
    count = lax.axis_size(axis)
    ends = count - 1
    head = lax.slice_in_dim(cells, 0, width, axis=dim)
    tail = lax.slice_in_dim(cells, cells.shape[dim] - width, cells.shape[dim], axis=dim)
    return jnp.concatenate(
        [
            lax.ppermute(tail, axis, [(i, (i + 1) % count) for i in range(ends)]),
            cells,
            lax.ppermute(head, axis, [((i + 1) % count, i) for i in range(ends)]),
        ],
        axis=dim,
    )


def embedded(bases, table):
    out = jnp.zeros(bases.shape + (table.shape[1],), jnp.float32)
    for v in range(table.shape[0]):
        out = out + jnp.where(bases[..., None] == v, table[v], 0.0)
    return out


def gather_blocks(block, bits, me):
    cur = block[None]
    for bit in reversed(range(bits)):
        other = partner(cur, "ch", bit)
        low = ((me >> bit) & 1) == 0
        first = jnp.where(low, cur, other)
        second = jnp.where(low, other, cur)
        cur = jnp.stack([first, second], axis=1).reshape((-1,) + block.shape)
    return cur


def scatter_blocks(part, bits, me):
    cur = part
    rows, _, w = part.shape
    for bit in range(bits):
        cur = cur.reshape(rows, -1, 2, w)
        low = ((me >> bit) & 1) == 0
        keep = jnp.where(low, cur[:, :, 0], cur[:, :, 1])
        give = jnp.where(low, cur[:, :, 1], cur[:, :, 0])
        cur = keep + partner(give.astype(jnp.bfloat16), "ch", bit).astype(jnp.float32)
    return cur[:, 0]


def flip_rows(values):
    batch, rows, _ = values.shape
    turn = jnp.broadcast_to(reversal(rows, rows), (batch, rows, rows))
    return lax.dot_general(
        turn, values, (((2,), (1,)), ((0,), (0,))), preferred_element_type=jnp.float32
    ).astype(jnp.bfloat16)


def reversal(n, block):
    rows = lax.broadcasted_iota(jnp.int32, (n, n), 0)
    cols = lax.broadcasted_iota(jnp.int32, (n, n), 1)
    same = rows // block == cols // block
    return (same & (rows % block + cols % block == block - 1)).astype(jnp.bfloat16)


def local(
    tokens,
    masked,
    hidden_forward,
    hidden_reverse,
    embed_table,
    conv_kernel,
    conv_bias,
    norm_gain,
    w_gate,
    w_value,
    w_out,
):
    seq_count = lax.axis_size("seq")
    ch_count = lax.axis_size("ch")
    ch_bits = ch_count.bit_length() - 1
    me = lax.axis_index("ch")
    table = embed_table.astype(jnp.float32)
    base_in = jnp.where(masked == 1, 4, tokens)
    comp = jnp.where(masked == 1, 4, 3 - tokens)
    comp_back = jnp.flip(mirror(comp, "seq", seq_count), axis=1)

    local_width = hidden_forward.shape[-1]
    width = local_width * ch_count
    taps = conv_kernel.shape[0]
    half_width = taps // 2

    x_fwd = hidden_forward.astype(jnp.float32) + embedded(base_in, table)
    x_rev = lax.optimization_barrier(hidden_reverse.astype(jnp.float32) + embedded(comp_back, table))
    square_fwd, square_rev = lax.psum(
        (jnp.sum(x_fwd * x_fwd, axis=-1), jnp.sum(x_rev * x_rev, axis=-1)), "ch"
    )
    normed_fwd = (x_fwd * lax.rsqrt(square_fwd[..., None] / width + 1e-05) * norm_gain).astype(
        jnp.bfloat16
    )
    normed_rev = (x_rev * lax.rsqrt(square_rev[..., None] / width + 1e-05) * norm_gain).astype(
        jnp.bfloat16
    )
    stacked = jnp.stack([normed_fwd, normed_rev])
    length = stacked.shape[2]
    padded = padded_2(stacked, "seq", 2, half_width).astype(jnp.float32)
    conv = jnp.zeros(stacked.shape, jnp.float32) + conv_bias
    for offset in range(taps):
        conv = conv + conv_kernel[offset] * padded[:, :, offset : offset + length]
    conv = conv.astype(jnp.bfloat16)
    rows_fwd = conv[0].reshape(-1, local_width)
    rows_all = rows_fwd.shape[0]
    rows_rev = mirror(
        flip_rows(conv[1]).reshape(rows_all, -1),
        "seq",
        seq_count,
    )

    def activation(rows):
        pieces = gather_blocks(rows, ch_bits, me)
        dims = (((0, 2), (0, 1)), ((), ()))
        gate = lax.dot_general(
            pieces, w_gate.reshape(ch_count, local_width, -1), dims, preferred_element_type=jnp.float32
        )
        value = lax.dot_general(
            pieces, w_value.reshape(ch_count, local_width, -1), dims, preferred_element_type=jnp.float32
        )
        return (jax.nn.silu(gate) * value).astype(jnp.bfloat16)

    act_fwd = activation(rows_fwd)
    act_rev = activation(rows_rev)
    lane_flip = reversal(local_width, local_width)
    w_flip = jnp.dot(w_out, reversal(width, width), preferred_element_type=jnp.float32).astype(jnp.bfloat16)
    part = jnp.dot(act_fwd, w_out, preferred_element_type=jnp.float32) + jnp.dot(
        act_rev, w_flip, preferred_element_type=jnp.float32
    )
    share = scatter_blocks(part.reshape(part.shape[0], ch_count, local_width), ch_bits, me)
    out_forward = x_fwd + share.reshape(x_fwd.shape)
    turned = jnp.dot(share.astype(jnp.bfloat16), lane_flip, preferred_element_type=jnp.float32)
    turned = flip_rows(turned.astype(jnp.bfloat16).reshape(x_fwd.shape))
    sent = mirror(turned, ("seq", "ch"), seq_count * ch_count)
    out_reverse = x_rev + sent.astype(jnp.float32)
    return (out_forward.astype(jnp.bfloat16), out_reverse.astype(jnp.bfloat16))


def solution(mesh):
    placed = (
        P(None, "seq"),
        P(None, "seq"),
        P(None, "seq", "ch"),
        P(None, "seq", "ch"),
        P(None, "ch"),
        P(None, "ch"),
        P("ch"),
        P("ch"),
        P(None, "ch"),
        P(None, "ch"),
        P("ch", None),
    )
    return jax.shard_map(
        local,
        mesh=mesh,
        in_specs=placed,
        out_specs=(P(None, "seq", "ch"), P(None, "seq", "ch")),
        check_vma=False,
    )
```
